256 devices in a mesh: tm: 32 (over y, x, core), state: 8 (over z).
Axes of the slice: x: 4, y: 4, z: 8, core: 2. Of those that a mesh axis runs over, the one named last changes fastest.
Arguments:
- solution: float32 [32, 96, 8192], P('tm', None, 'state'), may hold values from -6 to 6
- kernel: bfloat16 [256, 32, 128, 128], P('state', 'tm'), may hold values from -0.0625 to 0.0625
- pattern: int32 [256, 2], P('state'), may hold values from 0 to 63, as said below
- offsets: int32 [2], replicated, may hold values from 8 to 23, as said below
Outputs:
- field: float32 [32, 96, 8192], P('tm', None, 'state')
The draws below stay inside these ranges and needn't reach their ends.
Inputs may be any that keep to these rules, and one draw needn't show every extreme that they name: `pattern`: entries 32 * j to 32 * (j + 1) - 1 have row blocks among j * 8 to (j + 1) * 8 - 1; column blocks may be any, some much more common than others; a pair may repeat, and repeated blocks add. offsets[0] lies in [8, 16), and offsets[1] is 23.
All inputs are finite; a program needn't handle non-finite values.
Results may differ from the reference program's by a relative error of at most 0.0031.
Values may be sent and summed in bfloat16 or wider, within the bound.
No kernel may reach another device: no remote copies, remote signals or barrier semaphores. Data moves between devices by JAX's collectives and lax.ppermute only.
A program may use at most 64 MiB of HBM per device.

```python
import jax
import jax.numpy as jnp
from jax import lax

BLK = 128
RB_DEV = 8
COLS = 96
NNZ_DEV = 32
LEVELS = 2
NT = 32
STATES = 8192
NBLK = 64
NNZ = 256


def draw_pattern(key, part):
    keys = jax.random.split(jax.random.fold_in(key, 11), 5)
    owner_index = jnp.arange(NNZ, dtype=jnp.int32) // NNZ_DEV
    row_block = owner_index * RB_DEV + jax.random.randint(keys[0], (NNZ,), 0, RB_DEV, dtype=jnp.int32)
    first_draw = jax.random.randint(keys[1], (NNZ,), 0, NBLK, dtype=jnp.int32)
    second_draw = jax.random.randint(keys[2], (NNZ,), 0, NBLK, dtype=jnp.int32)
    rotation = jax.random.randint(keys[3], (), 0, NBLK, dtype=jnp.int32)
    coin_flip = jax.random.randint(keys[4], (NNZ,), 0, 2, dtype=jnp.int32)
    skewed = (first_draw * second_draw // NBLK + rotation) % NBLK
    col_block = jnp.where(coin_flip == 1, skewed, second_draw)
    return jnp.stack([row_block, col_block], axis=1).astype(jnp.int32)


def draw_offsets(key, part):
    quarter = NT // 4
    first_offset = quarter + jax.random.randint(jax.random.fold_in(key, 23), (1,), 0, quarter, dtype=jnp.int32)
    second_offset = jnp.full((1,), 3 * quarter - 1, dtype=jnp.int32)
    return jnp.concatenate([first_offset, second_offset]).astype(jnp.int32)


def levels(own_key, dims, shards, least, high):
    def one(axis_at, parts):
        heights = jax.random.uniform(jax.random.fold_in(jax.random.fold_in(own_key, 6), axis_at), (parts,), jnp.float32, least / len(shards), high / len(shards))
        return jnp.repeat(jnp.exp(heights), dims[axis_at] // parts).reshape((-1,) + (1,) * (len(dims) - axis_at - 1))

    level = one(*shards[0])
    for cut in shards[1:]:
        level = level * one(*cut)
    return level


def scatter_about(stream_key, extent, deviation, limit, cuts=(), kind=jnp.bfloat16):
    drawn = jax.random.normal(stream_key, extent, jnp.float32) * deviation
    if len(cuts) > 0:
        drawn = levels(stream_key, extent, cuts, -0.22, 0.18) * drawn
    return jnp.clip(drawn, min=-limit, max=limit).astype(kind)


def setup_inputs(seed: int = 0) -> dict:
    seeds = jax.random.split(jax.random.key(seed), 5)
    solution = scatter_about(seeds[0], (NT, COLS, STATES), 1.0, 6.0, ((0, 32), (2, 8)), jnp.float32)
    kernel = scatter_about(seeds[1], (NNZ, NT, BLK, BLK), (BLK * NNZ_DEV * NT // (2 * RB_DEV)) ** -0.5, 0.0625, ((0, 8), (1, 32)))
    pattern = draw_pattern(jax.random.fold_in(seeds[4], 71), 0)
    offsets = draw_offsets(jax.random.fold_in(seeds[4], 71), 0)
    return dict(solution=solution, kernel=kernel, pattern=pattern, offsets=offsets)


def reference(solution, kernel, pattern, offsets):
    times = jnp.arange(NT, dtype=jnp.int32)
    nblocks = STATES // BLK
    field = solution
    for level_index in range(LEVELS):
        boundary = offsets[level_index]
        left_part = jnp.where((times < boundary)[:, None, None], field, jnp.zeros_like(field))
        spectral_values = jnp.fft.fft(left_part, axis=0)
        spec_re = jnp.real(spectral_values).astype(jnp.bfloat16)
        spec_im = jnp.imag(spectral_values).astype(jnp.bfloat16)
        spec_re, spec_im = lax.optimization_barrier((spec_re, spec_im))
        spec_re = spec_re.astype(jnp.float32).reshape(NT, COLS, nblocks, BLK)
        spec_im = spec_im.astype(jnp.float32).reshape(NT, COLS, nblocks, BLK)

        def accumulate(carry, entry):
            total_re, total_im = carry
            row_block = pattern[entry, 0]
            col_block = pattern[entry, 1]
            kernel_spec = jnp.fft.fft(kernel[entry].astype(jnp.float32), axis=0)
            kernel_re = jnp.real(kernel_spec).astype(jnp.bfloat16)
            kernel_im = jnp.imag(kernel_spec).astype(jnp.bfloat16)
            kernel_re, kernel_im = lax.optimization_barrier((kernel_re, kernel_im))
            kernel_re = kernel_re.astype(jnp.float32)
            kernel_im = kernel_im.astype(jnp.float32)
            block_re = spec_re[:, :, col_block]
            block_im = spec_im[:, :, col_block]
            hp = lax.Precision.HIGHEST
            prod_re = jnp.einsum("fcj,frj->fcr", block_re, kernel_re, precision=hp) - jnp.einsum("fcj,frj->fcr", block_im, kernel_im, precision=hp)
            prod_im = jnp.einsum("fcj,frj->fcr", block_im, kernel_re, precision=hp) + jnp.einsum("fcj,frj->fcr", block_re, kernel_im, precision=hp)
            total_re = total_re.at[:, :, row_block].add(prod_re)
            total_im = total_im.at[:, :, row_block].add(prod_im)
            return (total_re, total_im), None

        zeros_block = jnp.zeros((NT, COLS, nblocks, BLK), jnp.float32)
        (total_re, total_im), _ = lax.scan(accumulate, (zeros_block, zeros_block), jnp.arange(NNZ, dtype=jnp.int32))
        response = jnp.real(jnp.fft.ifft(lax.complex(total_re, total_im), axis=0)).reshape(NT, COLS, STATES)
        field = field + jnp.where((times >= boundary)[:, None, None], response, jnp.zeros_like(response))
    return field
```

```python
import math

import jax
import jax.numpy as jnp
import numpy as np
from jax import lax
from jax.sharding import PartitionSpec as P

LEVELS = 2
HIGH = lax.Precision.HIGHEST


def slot_tables(length):
    half = length // 2
    t = np.arange(length)
    q = np.arange(half)
    angle = 2.0 * np.pi * np.outer(q, t) / length
    fwd_re = np.cos(angle)
    fwd_im = -np.sin(angle)
    fwd_re[0] = 1.0
    fwd_im[0] = np.cos(np.pi * t)
    inv_re = 2.0 * np.cos(angle.T) / length
    inv_im = -2.0 * np.sin(angle.T) / length
    inv_re[:, 0] = 1.0 / length
    inv_im[:, 0] = np.cos(np.pi * t) / length
    return tuple(jnp.asarray(a, jnp.float32) for a in (fwd_re, fwd_im, inv_re, inv_im))


def shards(solution, kernel, pattern, offsets):
    ntm = lax.axis_size("tm")
    nst = lax.axis_size("state")
    length = solution.shape[0] * ntm
    half = length // 2
    per_slot = ntm // half
    cols = solution.shape[1]
    states_local = solution.shape[2]
    nnz, _, block, _ = kernel.shape
    rows_local = states_local // block
    csl = cols // ntm
    sh = states_local // per_slot
    fwd_re, fwd_im, inv_re, inv_im = slot_tables(length)

    me = lax.axis_index("tm")
    my_state = lax.axis_index("state")
    my_slot = me // per_slot
    my_half = me % per_slot
    swap = [(i, i ^ 1) for i in range(ntm)]

    ksrc = kernel[:, 0].reshape(nnz, per_slot, ntm, block // (per_slot * ntm), block)
    ksrc = jnp.transpose(ksrc, (2, 0, 1, 3, 4))
    klags = lax.all_to_all(ksrc, "tm", 0, 0, tiled=True).astype(jnp.float32)
    kre = jnp.einsum("qt,tkhij->qhkij", fwd_re, klags, precision=HIGH).astype(jnp.bfloat16)
    kim = jnp.einsum("qt,tkhij->qhkij", fwd_im, klags, precision=HIGH).astype(jnp.bfloat16)
    kspec = jnp.stack([kre, kim], 2).reshape(ntm, 2, nnz, block // (per_slot * ntm), block)
    kspec = lax.all_to_all(kspec, "tm", 0, 0, tiled=True)
    kspec = jnp.transpose(kspec, (1, 2, 4, 0, 3)).reshape(2, nnz, block, block // per_slot)
    local_rows = pattern[:, 0] - my_state * rows_local
    selector = (local_rows[:, None] == jnp.arange(rows_local, dtype=jnp.int32)[None, :]).astype(
        jnp.bfloat16
    )
    ksel = kspec[:, :, :, None, :] * selector[None, :, None, :, None]
    ksel = ksel.reshape(2, nnz * block, rows_local * (block // per_slot))
    real_slot = (my_slot != 0).astype(jnp.float32)

    col_block = pattern[:, 1]
    blocks_half = rows_local // per_slot
    cb_state = col_block // rows_local
    cb_half = (col_block // blocks_half) % per_slot
    cb_blk = col_block % blocks_half
    cb_src = (cb_half != my_half).astype(jnp.int32)
    pick = cb_src * (nst * blocks_half) + cb_state * blocks_half + cb_blk

    def respond(left):
        xre = jnp.einsum("qt,tcn->qcn", fwd_re, left, precision=HIGH).astype(jnp.bfloat16)
        xim = jnp.einsum("qt,tcn->qcn", fwd_im, left, precision=HIGH).astype(jnp.bfloat16)
        xs = jnp.stack([xre, xim], 0).reshape(2, half, csl, per_slot, sh)
        xs = jnp.transpose(xs, (1, 3, 0, 2, 4)).reshape(ntm, 2, csl, sh)
        xs = lax.all_to_all(xs, "tm", 0, 0, tiled=True)
        xs = xs.reshape(ntm, 2, csl, blocks_half, block)
        xs = jnp.transpose(xs, (3, 1, 0, 2, 4)).reshape(blocks_half, 2, cols, block)
        mine = lax.all_gather(xs, "state", axis=0, tiled=False)
        other = lax.ppermute(mine, "tm", swap)
        whole = jnp.stack([mine, other], 0).reshape(per_slot * nst * blocks_half, 2, cols, block)
        picked = jnp.take(whole, pick, axis=0)
        picked = jnp.transpose(picked, (1, 2, 0, 3)).reshape(2, cols, nnz * block)
        prod = jnp.einsum("xck,ykd->xycd", picked, ksel, preferred_element_type=jnp.float32)
        a, c_, d, b = prod[0, 0], prod[0, 1], prod[1, 0], prod[1, 1]
        ys_re = a - real_slot * b
        ys_im = real_slot * (c_ + d) + (1.0 - real_slot) * b
        ys = jnp.stack([ys_re, ys_im], 0).reshape(2, ntm, csl, rows_local, block // per_slot)
        ys = jnp.transpose(ys, (1, 0, 2, 3, 4))
        ys = lax.all_to_all(ys, "tm", 0, 0, tiled=True)
        ys = ys.reshape(half, per_slot, 2, csl, rows_local, block // per_slot)
        ys = jnp.transpose(ys, (2, 0, 3, 4, 1, 5)).reshape(2, half, csl, states_local)
        return jnp.einsum("tq,qcn->tcn", inv_re, ys[0], precision=HIGH) + jnp.einsum(
            "tq,qcn->tcn", inv_im, ys[1], precision=HIGH
        )

    field = solution[0].reshape(ntm, csl, states_local)
    field = lax.all_to_all(field, "tm", 0, 0, tiled=True)
    times = jnp.arange(length, dtype=jnp.int32)[:, None, None]
    for level_index in range(LEVELS):
        boundary = offsets[level_index]
        left = jnp.where(times < boundary, field, 0.0)
        response = respond(left)
        field = field + jnp.where(times >= boundary, response, 0.0)
    field = lax.all_to_all(field, "tm", 0, 0, tiled=True)
    return field.reshape(1, cols, states_local)


def solution(mesh):
    return jax.shard_map(
        shards,
        mesh=mesh,
        in_specs=(P("tm", None, "state"), P("state", "tm", None, None), P("state", None), P()),
        out_specs=P("tm", None, "state"),
        check_vma=False,
    )
```

```python
import math

import jax
import jax.numpy as jnp
import numpy as np
from jax import lax
from jax.sharding import PartitionSpec as P

LEVELS = 2
HIGH = lax.Precision.HIGHEST


def slot_tables(length):
    half = length // 2
    t = np.arange(length)
    q = np.arange(half)
    angle = 2.0 * np.pi * np.outer(q, t) / length
    fwd_re = np.cos(angle)
    fwd_im = -np.sin(angle)
    fwd_re[0] = 1.0
    fwd_im[0] = np.cos(np.pi * t)
    inv_re = 2.0 * np.cos(angle.T) / length
    inv_im = -2.0 * np.sin(angle.T) / length
    inv_re[:, 0] = 1.0 / length
    inv_im[:, 0] = np.cos(np.pi * t) / length
    return tuple(jnp.asarray(a, jnp.float32) for a in (fwd_re, fwd_im, inv_re, inv_im))


def shards(solution, kernel, pattern, offsets):
    ntm = lax.axis_size("tm")
    nst = lax.axis_size("state")
    length = solution.shape[0] * ntm
    half = length // 2
    per_slot = ntm // half
    cols = solution.shape[1]
    states_local = solution.shape[2]
    nnz, _, block, _ = kernel.shape
    rows_local = states_local // block
    csl = cols // ntm
    sh = states_local // per_slot
    fwd_re, fwd_im, inv_re, inv_im = slot_tables(length)

    me = lax.axis_index("tm")
    my_state = lax.axis_index("state")
    my_slot = me // per_slot
    my_half = me % per_slot
    swap = [(i, i ^ 1) for i in range(ntm)]

    ksrc = kernel[:, 0].reshape(nnz, per_slot, ntm, block // (per_slot * ntm), block)
    ksrc = jnp.transpose(ksrc, (2, 0, 1, 3, 4))
    klags = lax.all_to_all(ksrc, "tm", 0, 0, tiled=True).astype(jnp.float32)
    kre = jnp.einsum("qt,tkhij->qhkij", fwd_re, klags, precision=HIGH).astype(jnp.bfloat16)
    kim = jnp.einsum("qt,tkhij->qhkij", fwd_im, klags, precision=HIGH).astype(jnp.bfloat16)
    kspec = jnp.stack([kre, kim], 2).reshape(ntm, 2, nnz, block // (per_slot * ntm), block)
    kspec = lax.all_to_all(kspec, "tm", 0, 0, tiled=True)
    local_rows = pattern[:, 0] - my_state * rows_local
    selector = (local_rows[:, None] == jnp.arange(rows_local, dtype=jnp.int32)[None, :]).astype(
        jnp.float32
    )
    kspec = jnp.transpose(kspec, (1, 2, 0, 3, 4)).reshape(2, nnz, block // per_slot, block)
    real_slot = (my_slot != 0).astype(jnp.float32)

    col_block = pattern[:, 1]
    blocks_half = rows_local // per_slot
    rel = (col_block // rows_local - my_state) % nst
    rel = jnp.where(rel < nst // 2, rel, rel - nst)
    position = jnp.where(rel > 0, 2 * rel, -2 * rel - 1)
    position = jnp.where(rel == 0, 0, position)
    cb_half = (col_block // blocks_half) % per_slot
    cb_src = (cb_half != my_half).astype(jnp.int32)
    pick = cb_src * (nst * blocks_half) + position * blocks_half + col_block % blocks_half
    fwd = [(i, (i + 1) % nst) for i in range(nst)]
    bwd = [(i, (i - 1) % nst) for i in range(nst)]

    def ring_gather(x):
        parts = [x]
        a = x
        b = x
        for step in range(1, nst // 2 + 1):
            a = lax.ppermute(a, "state", fwd)
            parts.append(a)
            if step < nst // 2:
                b = lax.ppermute(b, "state", bwd)
                parts.append(b)
        return jnp.stack(parts, 0)

    def respond(left):
        xre = jnp.einsum("qt,tcn->qcn", fwd_re, left, precision=HIGH).astype(jnp.bfloat16)
        xim = jnp.einsum("qt,tcn->qcn", fwd_im, left, precision=HIGH).astype(jnp.bfloat16)
        xs = jnp.stack([xre, xim], 0).reshape(2, half, csl, per_slot, sh)
        xs = jnp.transpose(xs, (1, 3, 0, 2, 4)).reshape(ntm, 2, csl, sh)
        xs = lax.all_to_all(xs, "tm", 0, 0, tiled=True)
        xs = xs.reshape(ntm, 2, csl, blocks_half, block)
        xs = jnp.transpose(xs, (3, 1, 0, 2, 4)).reshape(blocks_half, 2, cols, block)
        mine = ring_gather(xs)
        other = lax.ppermute(mine, "tm", swap)
        whole = jnp.stack([mine, other], 0).reshape(per_slot * nst * blocks_half, 2, cols, block)
        picked = jnp.take(whole, pick, axis=0)
        prod = jnp.einsum("kxcj,ykaj->xykca", picked, kspec, preferred_element_type=jnp.float32)
        prod = jnp.einsum("xykca,kr->xycra", prod, selector, precision=HIGH)
        prod = prod.reshape(2, 2, cols, rows_local * (block // per_slot))
        a, c_, d, b = prod[0, 0], prod[0, 1], prod[1, 0], prod[1, 1]
        ys_re = a - real_slot * b
        ys_im = real_slot * (c_ + d) + (1.0 - real_slot) * b
        ys = jnp.stack([ys_re, ys_im], 0).reshape(2, ntm, csl, rows_local, block // per_slot)
        ys = jnp.transpose(ys, (1, 0, 2, 3, 4))
        ys = lax.all_to_all(ys, "tm", 0, 0, tiled=True)
        ys = ys.reshape(half, per_slot, 2, csl, rows_local, block // per_slot)
        ys = jnp.transpose(ys, (2, 0, 3, 4, 1, 5)).reshape(2, half, csl, states_local)
        return jnp.einsum("tq,qcn->tcn", inv_re, ys[0], precision=HIGH) + jnp.einsum(
            "tq,qcn->tcn", inv_im, ys[1], precision=HIGH
        )

    field = solution[0].reshape(ntm, csl, states_local)
    field = lax.all_to_all(field, "tm", 0, 0, tiled=True)
    times = jnp.arange(length, dtype=jnp.int32)[:, None, None]
    for level_index in range(LEVELS):
        boundary = offsets[level_index]
        left = jnp.where(times < boundary, field, 0.0)
        response = respond(left)
        field = field + jnp.where(times >= boundary, response, 0.0)
    field = lax.all_to_all(field, "tm", 0, 0, tiled=True)
    return field.reshape(1, cols, states_local)


def solution(mesh):
    return jax.shard_map(
        shards,
        mesh=mesh,
        in_specs=(P("tm", None, "state"), P("state", "tm", None, None), P("state", None), P()),
        out_specs=P("tm", None, "state"),
        check_vma=False,
    )
```

```python
import math

import jax
import jax.numpy as jnp
import numpy as np
from jax import lax
from jax.sharding import PartitionSpec as P

LEVELS = 2
HIGH = lax.Precision.HIGHEST


def slot_tables(length):
    half = length // 2
    t = np.arange(length)
    q = np.arange(half)
    angle = 2.0 * np.pi * np.outer(q, t) / length
    fwd_re = np.cos(angle)
    fwd_im = -np.sin(angle)
    fwd_re[0] = 1.0
    fwd_im[0] = np.cos(np.pi * t)
    inv_re = 2.0 * np.cos(angle.T) / length
    inv_im = -2.0 * np.sin(angle.T) / length
    inv_re[:, 0] = 1.0 / length
    inv_im[:, 0] = np.cos(np.pi * t) / length
    return tuple(jnp.asarray(a, jnp.float32) for a in (fwd_re, fwd_im, inv_re, inv_im))


def shards(solution, kernel, pattern, offsets):
    ntm = lax.axis_size("tm")
    nst = lax.axis_size("state")
    length = solution.shape[0] * ntm
    half = length // 2
    per_slot = ntm // half
    cols = solution.shape[1]
    states_local = solution.shape[2]
    nnz, _, block, _ = kernel.shape
    rows_local = states_local // block
    csl = cols // ntm
    sh = states_local // per_slot
    fwd_re, fwd_im, inv_re, inv_im = slot_tables(length)

    me = lax.axis_index("tm")
    my_state = lax.axis_index("state")
    my_slot = me // per_slot
    my_half = me % per_slot
    swap = [(i, i ^ 1) for i in range(ntm)]

    ksrc = kernel[:, 0].reshape(nnz, per_slot, ntm, block // (per_slot * ntm), block)
    ksrc = jnp.transpose(ksrc, (2, 0, 1, 3, 4))
    local_rows = pattern[:, 0] - my_state * rows_local
    selector = (local_rows[:, None] == jnp.arange(rows_local, dtype=jnp.int32)[None, :]).astype(
        jnp.float32
    )
    real_slot = (my_slot != 0).astype(jnp.float32)

    col_block = pattern[:, 1]
    blocks_half = rows_local // per_slot
    rel = (col_block // rows_local - my_state) % nst
    rel = jnp.where(rel < nst // 2, rel, rel - nst)
    position = jnp.where(rel > 0, 2 * rel, -2 * rel - 1)
    position = jnp.where(rel == 0, 0, position)
    cb_half = (col_block // blocks_half) % per_slot
    from_other = cb_half != my_half
    pick = position * blocks_half + col_block % blocks_half
    fwd = [(i, (i + 1) % nst) for i in range(nst)]
    bwd = [(i, (i - 1) % nst) for i in range(nst)]

    def ring_gather(x):
        parts = [x]
        a = x
        b = x
        for step in range(1, nst // 2 + 1):
            a = lax.ppermute(a, "state", fwd)
            parts.append(a)
            if step < nst // 2:
                b = lax.ppermute(b, "state", bwd)
                parts.append(b)
        return jnp.stack(parts, 0)

    def kernel_spectrum(klags):
        klags = klags.astype(jnp.float32)
        kre = jnp.einsum("qt,tkhij->qhkij", fwd_re, klags, precision=HIGH).astype(jnp.bfloat16)
        kim = jnp.einsum("qt,tkhij->qhkij", fwd_im, klags, precision=HIGH).astype(jnp.bfloat16)
        kspec = jnp.stack([kre, kim], 2).reshape(ntm, 2, nnz, block // (per_slot * ntm), block)
        kspec = lax.all_to_all(kspec, "tm", 0, 0, tiled=True)
        return jnp.transpose(kspec, (1, 2, 0, 3, 4)).reshape(2, nnz, block // per_slot, block)

    def respond(left, kspec):
        xre = jnp.einsum("qt,tcn->qcn", fwd_re, left, precision=HIGH).astype(jnp.bfloat16)
        xim = jnp.einsum("qt,tcn->qcn", fwd_im, left, precision=HIGH).astype(jnp.bfloat16)
        xs = jnp.stack([xre, xim], 0).reshape(2, half, csl, per_slot, sh)
        xs = jnp.transpose(xs, (1, 3, 0, 2, 4)).reshape(ntm, 2, csl, sh)
        if kspec is None:
            both = jnp.concatenate([xs.reshape(ntm, -1), ksrc.reshape(ntm, -1)], 1)
            both = lax.all_to_all(both, "tm", 0, 0, tiled=True)
            xs = both[:, : xs[0].size].reshape(xs.shape)
            kspec = kernel_spectrum(both[:, xs[0].size :].reshape(ksrc.shape))
        else:
            xs = lax.all_to_all(xs, "tm", 0, 0, tiled=True)
        xs = xs.reshape(ntm, 2, csl, blocks_half, block)
        xs = jnp.transpose(xs, (3, 1, 0, 2, 4)).reshape(blocks_half, 2, cols, block)
        mine = ring_gather(xs)
        other = lax.ppermute(mine, "tm", swap)
        mine = mine.reshape(nst * blocks_half, 2, cols, block)
        other = other.reshape(nst * blocks_half, 2, cols, block)
        picked = jnp.where(
            from_other[:, None, None, None], jnp.take(other, pick, axis=0), jnp.take(mine, pick, axis=0)
        )
        prod = jnp.einsum("kxcj,ykaj->xykca", picked, kspec, preferred_element_type=jnp.float32)
        prod = jnp.einsum("xykca,kr->xycra", prod, selector, precision=HIGH)
        prod = prod.reshape(2, 2, cols, rows_local * (block // per_slot))
        a, c_, d, b = prod[0, 0], prod[0, 1], prod[1, 0], prod[1, 1]
        ys_re = a - real_slot * b
        ys_im = real_slot * (c_ + d) + (1.0 - real_slot) * b
        ys = jnp.stack([ys_re, ys_im], 0).reshape(2, ntm, csl, rows_local, block // per_slot)
        ys = jnp.transpose(ys, (1, 0, 2, 3, 4))
        ys = lax.all_to_all(ys, "tm", 0, 0, tiled=True)
        ys = ys.reshape(half, per_slot, 2, csl, rows_local, block // per_slot)
        ys = jnp.transpose(ys, (2, 0, 3, 4, 1, 5)).reshape(2, half, csl, states_local)
        response = jnp.einsum("tq,qcn->tcn", inv_re, ys[0], precision=HIGH) + jnp.einsum(
            "tq,qcn->tcn", inv_im, ys[1], precision=HIGH
        )
        return response, kspec

    field = solution[0].reshape(ntm, csl, states_local)
    field = lax.all_to_all(field, "tm", 0, 0, tiled=True)
    times = jnp.arange(length, dtype=jnp.int32)[:, None, None]
    kspec = None
    for level_index in range(LEVELS):
        boundary = offsets[level_index]
        left = jnp.where(times < boundary, field, 0.0)
        response, kspec = respond(left, kspec)
        field = field + jnp.where(times >= boundary, response, 0.0)
    field = lax.all_to_all(field, "tm", 0, 0, tiled=True)
    return field.reshape(1, cols, states_local)


def solution(mesh):
    return jax.shard_map(
        shards,
        mesh=mesh,
        in_specs=(P("tm", None, "state"), P("state", "tm", None, None), P("state", None), P()),
        out_specs=P("tm", None, "state"),
        check_vma=False,
    )
```

```python
import math

import jax
import jax.numpy as jnp
import numpy as np
from jax import lax
from jax.experimental import pallas as pl
from jax.experimental.pallas import tpu as pltpu
from jax.sharding import PartitionSpec as P

LEVELS = 2
HIGH = lax.Precision.HIGHEST


def slot_tables(length):
    half = length // 2
    t = np.arange(length)
    q = np.arange(half)
    angle = 2.0 * np.pi * np.outer(q, t) / length
    fwd_re = np.cos(angle)
    fwd_im = -np.sin(angle)
    fwd_re[0] = 1.0
    fwd_im[0] = np.cos(np.pi * t)
    inv_re = 2.0 * np.cos(angle.T) / length
    inv_im = -2.0 * np.sin(angle.T) / length
    inv_re[:, 0] = 1.0 / length
    inv_im[:, 0] = np.cos(np.pi * t) / length
    return tuple(jnp.asarray(a, jnp.float32) for a in (fwd_re, fwd_im, inv_re, inv_im))


def _products_body(pick_ref, src_ref, row_ref, mine_ref, other_ref, kk_ref, out_ref):
    out_ref[...] = jnp.zeros_like(out_ref)

    def step(k, carry):
        p = pick_ref[k]
        x = jnp.where(src_ref[k] == 1, other_ref[p], mine_ref[p])
        prod = lax.dot_general(
            x, kk_ref[k], (((1,), (1,)), ((), ())), preferred_element_type=jnp.float32
        )
        r = row_ref[k]
        out_ref[r] = out_ref[r] + prod
        return carry

    lax.fori_loop(0, kk_ref.shape[0], step, 0)


def block_products(pick, src, row, mine, other, kk, rows_local):
    nblk, m, j = mine.shape
    nnz, n, _ = kk.shape
    full = lambda *shape: pl.BlockSpec(shape, lambda i, *_: (0,) * len(shape))
    return pl.pallas_call(
        _products_body,
        grid_spec=pltpu.PrefetchScalarGridSpec(
            num_scalar_prefetch=3,
            grid=(1,),
            in_specs=[full(nblk, m, j), full(nblk, m, j), full(nnz, n, j)],
            out_specs=full(rows_local, m, n),
        ),
        out_shape=jax.ShapeDtypeStruct((rows_local, m, n), jnp.float32),
    )(pick, src, row, mine, other, kk)


def shards(solution, kernel, pattern, offsets):
    ntm = lax.axis_size("tm")
    nst = lax.axis_size("state")
    length = solution.shape[0] * ntm
    half = length // 2
    per_slot = ntm // half
    cols = solution.shape[1]
    states_local = solution.shape[2]
    nnz, _, block, _ = kernel.shape
    rows_local = states_local // block
    csl = cols // ntm
    sh = states_local // per_slot
    fwd_re, fwd_im, inv_re, inv_im = slot_tables(length)

    me = lax.axis_index("tm")
    my_state = lax.axis_index("state")
    my_slot = me // per_slot
    my_half = me % per_slot
    swap = [(i, i ^ 1) for i in range(ntm)]

    ksrc = kernel[:, 0].reshape(nnz, per_slot, ntm, block // (per_slot * ntm), block)
    ksrc = jnp.transpose(ksrc, (2, 0, 1, 3, 4))
    klags = lax.all_to_all(ksrc, "tm", 0, 0, tiled=True).astype(jnp.float32)
    kre = jnp.einsum("qt,tkhij->qhkij", fwd_re, klags, precision=HIGH).astype(jnp.bfloat16)
    kim = jnp.einsum("qt,tkhij->qhkij", fwd_im, klags, precision=HIGH).astype(jnp.bfloat16)
    kspec = jnp.stack([kre, kim], 2).reshape(ntm, 2, nnz, block // (per_slot * ntm), block)
    kspec = lax.all_to_all(kspec, "tm", 0, 0, tiled=True)
    local_rows = pattern[:, 0] - my_state * rows_local
    kk = jnp.transpose(kspec, (2, 1, 0, 3, 4)).reshape(nnz, block, block)
    row_of = jnp.clip(local_rows, 0, rows_local - 1)
    real_slot = (my_slot != 0).astype(jnp.float32)

    col_block = pattern[:, 1]
    blocks_half = rows_local // per_slot
    rel = (col_block // rows_local - my_state) % nst
    rel = jnp.where(rel < nst // 2, rel, rel - nst)
    position = jnp.where(rel > 0, 2 * rel, -2 * rel - 1)
    position = jnp.where(rel == 0, 0, position)
    cb_half = (col_block // blocks_half) % per_slot
    cb_src = (cb_half != my_half).astype(jnp.int32)
    pick = position * blocks_half + col_block % blocks_half
    fwd = [(i, (i + 1) % nst) for i in range(nst)]
    bwd = [(i, (i - 1) % nst) for i in range(nst)]

    def ring_gather(x):
        parts = [x]
        a = x
        b = x
        for step in range(1, nst // 2 + 1):
            a = lax.ppermute(a, "state", fwd)
            parts.append(a)
            if step < nst // 2:
                b = lax.ppermute(b, "state", bwd)
                parts.append(b)
        return jnp.stack(parts, 0)

    def respond(left):
        xre = jnp.einsum("qt,tcn->qcn", fwd_re, left, precision=HIGH).astype(jnp.bfloat16)
        xim = jnp.einsum("qt,tcn->qcn", fwd_im, left, precision=HIGH).astype(jnp.bfloat16)
        xs = jnp.stack([xre, xim], 0).reshape(2, half, csl, per_slot, sh)
        xs = jnp.transpose(xs, (1, 3, 0, 2, 4)).reshape(ntm, 2, csl, sh)
        xs = lax.all_to_all(xs, "tm", 0, 0, tiled=True)
        xs = xs.reshape(ntm, 2, csl, blocks_half, block)
        xs = jnp.transpose(xs, (3, 1, 0, 2, 4)).reshape(blocks_half, 2, cols, block)
        mine = ring_gather(xs)
        other = lax.ppermute(mine, "tm", swap)
        mine = mine.reshape(nst * blocks_half, 2 * cols, block)
        other = other.reshape(nst * blocks_half, 2 * cols, block)
        prod = block_products(pick, cb_src, row_of, mine, other, kk, rows_local)
        ah = block // per_slot
        a, c_ = prod[:, :cols, :ah], prod[:, :cols, ah:]
        d, b = prod[:, cols:, :ah], prod[:, cols:, ah:]
        ys_re = a - real_slot * b
        ys_im = real_slot * (c_ + d) + (1.0 - real_slot) * b
        ys_re = jnp.transpose(ys_re, (1, 0, 2)).reshape(cols, rows_local * ah)
        ys_im = jnp.transpose(ys_im, (1, 0, 2)).reshape(cols, rows_local * ah)
        ys = jnp.stack([ys_re, ys_im], 0).reshape(2, ntm, csl, rows_local, block // per_slot)
        ys = jnp.transpose(ys, (1, 0, 2, 3, 4))
        ys = lax.all_to_all(ys, "tm", 0, 0, tiled=True)
        ys = ys.reshape(half, per_slot, 2, csl, rows_local, block // per_slot)
        ys = jnp.transpose(ys, (2, 0, 3, 4, 1, 5)).reshape(2, half, csl, states_local)
        return jnp.einsum("tq,qcn->tcn", inv_re, ys[0], precision=HIGH) + jnp.einsum(
            "tq,qcn->tcn", inv_im, ys[1], precision=HIGH
        )

    field = solution[0].reshape(ntm, csl, states_local)
    field = lax.all_to_all(field, "tm", 0, 0, tiled=True)
    times = jnp.arange(length, dtype=jnp.int32)[:, None, None]
    for level_index in range(LEVELS):
        boundary = offsets[level_index]
        left = jnp.where(times < boundary, field, 0.0)
        response = respond(left)
        field = field + jnp.where(times >= boundary, response, 0.0)
    field = lax.all_to_all(field, "tm", 0, 0, tiled=True)
    return field.reshape(1, cols, states_local)


def solution(mesh):
    return jax.shard_map(
        shards,
        mesh=mesh,
        in_specs=(P("tm", None, "state"), P("state", "tm", None, None), P("state", None), P()),
        out_specs=P("tm", None, "state"),
        check_vma=False,
    )
```

```python
import math

import jax
import jax.numpy as jnp
import numpy as np
from jax import lax
from jax.experimental import pallas as pl
from jax.experimental.pallas import tpu as pltpu
from jax.sharding import PartitionSpec as P

LEVELS = 2
HIGH = lax.Precision.HIGHEST


def slot_tables(length):
    half = length // 2
    t = np.arange(length)
    q = np.arange(half)
    angle = 2.0 * np.pi * np.outer(q, t) / length
    fwd_re = np.cos(angle)
    fwd_im = -np.sin(angle)
    fwd_re[0] = 1.0
    fwd_im[0] = np.cos(np.pi * t)
    inv_re = 2.0 * np.cos(angle.T) / length
    inv_im = -2.0 * np.sin(angle.T) / length
    inv_re[:, 0] = 1.0 / length
    inv_im[:, 0] = np.cos(np.pi * t) / length
    return tuple(jnp.asarray(a, jnp.float32) for a in (fwd_re, fwd_im, inv_re, inv_im))


def _products_body(pick_ref, src_ref, row_ref, mine_ref, other_ref, kk_ref, out_ref):
    out_ref[...] = jnp.zeros_like(out_ref)

    def step(k, carry):
        p = pick_ref[k]
        x = jnp.where(src_ref[k] == 1, other_ref[p], mine_ref[p])
        prod = lax.dot_general(
            x, kk_ref[k], (((1,), (1,)), ((), ())), preferred_element_type=jnp.float32
        )
        r = row_ref[k]
        out_ref[r] = out_ref[r] + prod
        return carry

    lax.fori_loop(0, kk_ref.shape[0], step, 0)


def block_products(pick, src, row, mine, other, kk, rows_local):
    nblk, m, j = mine.shape
    nnz, n, _ = kk.shape
    full = lambda *shape: pl.BlockSpec(shape, lambda i, *_: (0,) * len(shape))
    return pl.pallas_call(
        _products_body,
        grid_spec=pltpu.PrefetchScalarGridSpec(
            num_scalar_prefetch=3,
            grid=(1,),
            in_specs=[full(nblk, m, j), full(nblk, m, j), full(nnz, n, j)],
            out_specs=full(rows_local, m, n),
        ),
        out_shape=jax.ShapeDtypeStruct((rows_local, m, n), jnp.float32),
    )(pick, src, row, mine, other, kk)


def shards(solution, kernel, pattern, offsets):
    ntm = lax.axis_size("tm")
    nst = lax.axis_size("state")
    length = solution.shape[0] * ntm
    half = length // 2
    per_slot = ntm // half
    cols = solution.shape[1]
    states_local = solution.shape[2]
    nnz, _, block, _ = kernel.shape
    rows_local = states_local // block
    csl = cols // ntm
    sh = states_local // per_slot
    fwd_re, fwd_im, inv_re, inv_im = slot_tables(length)

    me = lax.axis_index("tm")
    my_state = lax.axis_index("state")
    my_slot = me // per_slot
    my_half = me % per_slot
    swap = [(i, i ^ 1) for i in range(ntm)]

    ksrc = kernel[:, 0].reshape(nnz, per_slot, ntm, block // (per_slot * ntm), block)
    ksrc = jnp.transpose(ksrc, (2, 0, 1, 3, 4))
    klags = lax.all_to_all(ksrc, "tm", 0, 0, tiled=True).astype(jnp.float32)
    kre = jnp.einsum("qt,tkhij->qhkij", fwd_re, klags, precision=HIGH).astype(jnp.bfloat16)
    kim = jnp.einsum("qt,tkhij->qhkij", fwd_im, klags, precision=HIGH).astype(jnp.bfloat16)
    kspec = jnp.stack([kre, kim], 2).reshape(ntm, 2, nnz, block // (per_slot * ntm), block)
    kspec = lax.all_to_all(kspec, "tm", 0, 0, tiled=True)
    local_rows = pattern[:, 0] - my_state * rows_local
    kk = jnp.transpose(kspec, (2, 1, 0, 3, 4)).reshape(nnz, block, block)
    row_of = jnp.clip(local_rows, 0, rows_local - 1)
    real_slot = (my_slot != 0).astype(jnp.float32)

    col_block = pattern[:, 1]
    blocks_half = rows_local // per_slot
    rel = (col_block // rows_local - my_state) % nst
    rel = jnp.where(rel < nst // 2, rel, rel - nst)
    position = jnp.where(rel > 0, 2 * rel, -2 * rel - 1)
    position = jnp.where(rel == 0, 0, position)
    cb_half = (col_block // blocks_half) % per_slot
    cb_src = (cb_half != my_half).astype(jnp.int32)
    pick_ring = position * blocks_half + col_block % blocks_half
    pick_ordered = (col_block // rows_local) * blocks_half + col_block % blocks_half
    fwd = [(i, (i + 1) % nst) for i in range(nst)]
    bwd = [(i, (i - 1) % nst) for i in range(nst)]

    def ring_gather(x):
        parts = [x]
        a = x
        b = x
        for step in range(1, nst // 2 + 1):
            a = lax.ppermute(a, "state", fwd)
            parts.append(a)
            if step < nst // 2:
                b = lax.ppermute(b, "state", bwd)
                parts.append(b)
        return jnp.stack(parts, 0)

    def respond(left, on_ring):
        xre = jnp.einsum("qt,tcn->qcn", fwd_re, left, precision=HIGH).astype(jnp.bfloat16)
        xim = jnp.einsum("qt,tcn->qcn", fwd_im, left, precision=HIGH).astype(jnp.bfloat16)
        xs = jnp.stack([xre, xim], 0).reshape(2, half, csl, per_slot, sh)
        xs = jnp.transpose(xs, (1, 3, 0, 2, 4)).reshape(ntm, 2, csl, sh)
        xs = lax.all_to_all(xs, "tm", 0, 0, tiled=True)
        xs = xs.reshape(ntm, 2, csl, blocks_half, block)
        xs = jnp.transpose(xs, (3, 1, 0, 2, 4)).reshape(blocks_half, 2, cols, block)
        if on_ring:
            mine = ring_gather(xs)
            pick = pick_ring
        else:
            mine = lax.all_gather(xs, "state", axis=0, tiled=False)
            pick = pick_ordered
        other = lax.ppermute(mine, "tm", swap)
        mine = mine.reshape(nst * blocks_half, 2 * cols, block)
        other = other.reshape(nst * blocks_half, 2 * cols, block)
        prod = block_products(pick, cb_src, row_of, mine, other, kk, rows_local)
        ah = block // per_slot
        a, c_ = prod[:, :cols, :ah], prod[:, :cols, ah:]
        d, b = prod[:, cols:, :ah], prod[:, cols:, ah:]
        ys_re = a - real_slot * b
        ys_im = real_slot * (c_ + d) + (1.0 - real_slot) * b
        ys_re = jnp.transpose(ys_re, (1, 0, 2)).reshape(cols, rows_local * ah)
        ys_im = jnp.transpose(ys_im, (1, 0, 2)).reshape(cols, rows_local * ah)
        ys = jnp.stack([ys_re, ys_im], 0).reshape(2, ntm, csl, rows_local, block // per_slot)
        ys = jnp.transpose(ys, (1, 0, 2, 3, 4))
        ys = lax.all_to_all(ys, "tm", 0, 0, tiled=True)
        ys = ys.reshape(half, per_slot, 2, csl, rows_local, block // per_slot)
        ys = jnp.transpose(ys, (2, 0, 3, 4, 1, 5)).reshape(2, half, csl, states_local)
        return jnp.einsum("tq,qcn->tcn", inv_re, ys[0], precision=HIGH) + jnp.einsum(
            "tq,qcn->tcn", inv_im, ys[1], precision=HIGH
        )

    field = solution[0].reshape(ntm, csl, states_local)
    field = lax.all_to_all(field, "tm", 0, 0, tiled=True)
    times = jnp.arange(length, dtype=jnp.int32)[:, None, None]
    for level_index in range(LEVELS):
        boundary = offsets[level_index]
        left = jnp.where(times < boundary, field, 0.0)
        response = respond(left, level_index > 0)
        field = field + jnp.where(times >= boundary, response, 0.0)
    field = lax.all_to_all(field, "tm", 0, 0, tiled=True)
    return field.reshape(1, cols, states_local)


def solution(mesh):
    return jax.shard_map(
        shards,
        mesh=mesh,
        in_specs=(P("tm", None, "state"), P("state", "tm", None, None), P("state", None), P()),
        out_specs=P("tm", None, "state"),
        check_vma=False,
    )
```

```python
import math

import jax
import jax.numpy as jnp
import numpy as np
from jax import lax
from jax.experimental import pallas as pl
from jax.experimental.pallas import tpu as pltpu
from jax.sharding import PartitionSpec as P

LEVELS = 2
HIGH = lax.Precision.HIGHEST


def slot_tables(length):
    half = length // 2
    t = np.arange(length)
    q = np.arange(half)
    angle = 2.0 * np.pi * np.outer(q, t) / length
    fwd_re = np.cos(angle)
    fwd_im = -np.sin(angle)
    fwd_re[0] = 1.0
    fwd_im[0] = np.cos(np.pi * t)
    inv_re = 2.0 * np.cos(angle.T) / length
    inv_im = -2.0 * np.sin(angle.T) / length
    inv_re[:, 0] = 1.0 / length
    inv_im[:, 0] = np.cos(np.pi * t) / length
    return tuple(jnp.asarray(a, jnp.float32) for a in (fwd_re, fwd_im, inv_re, inv_im))


def _products_body(pick_ref, src_ref, row_ref, mine_ref, other_ref, kk_ref, out_ref):
    out_ref[...] = jnp.zeros_like(out_ref)

    def step(k, carry):
        p = pick_ref[k]
        x = jnp.where(src_ref[k] == 1, other_ref[p], mine_ref[p])
        prod = lax.dot_general(
            x, kk_ref[k], (((1,), (1,)), ((), ())), preferred_element_type=jnp.float32
        )
        r = row_ref[k]
        out_ref[r] = out_ref[r] + prod
        return carry

    lax.fori_loop(0, kk_ref.shape[0], step, 0)


def block_products(pick, src, row, mine, other, kk, rows_local):
    nblk, m, j = mine.shape
    nnz, n, _ = kk.shape
    full = lambda *shape: pl.BlockSpec(shape, lambda i, *_: (0,) * len(shape))
    return pl.pallas_call(
        _products_body,
        grid_spec=pltpu.PrefetchScalarGridSpec(
            num_scalar_prefetch=3,
            grid=(1,),
            in_specs=[full(nblk, m, j), full(nblk, m, j), full(nnz, n, j)],
            out_specs=full(rows_local, m, n),
        ),
        out_shape=jax.ShapeDtypeStruct((rows_local, m, n), jnp.float32),
    )(pick, src, row, mine, other, kk)


def shards(solution, kernel, pattern, offsets):
    ntm = lax.axis_size("tm")
    nst = lax.axis_size("state")
    length = solution.shape[0] * ntm
    half = length // 2
    per_slot = ntm // half
    cols = solution.shape[1]
    states_local = solution.shape[2]
    nnz, _, block, _ = kernel.shape
    rows_local = states_local // block
    csl = cols // ntm
    sh = states_local // per_slot
    fwd_re, fwd_im, inv_re, inv_im = slot_tables(length)

    me = lax.axis_index("tm")
    my_state = lax.axis_index("state")
    my_slot = me // per_slot
    my_half = me % per_slot
    swap = [(i, i ^ 1) for i in range(ntm)]

    ksrc = kernel[:, 0].reshape(nnz, per_slot, ntm, block // (per_slot * ntm), block)
    ksrc = jnp.transpose(ksrc, (2, 0, 1, 3, 4))
    klags = lax.all_to_all(ksrc, "tm", 0, 0, tiled=True)
    klags, solution = lax.optimization_barrier((klags, solution))
    klags = klags.astype(jnp.float32)
    kre = jnp.einsum("qt,tkhij->qhkij", fwd_re, klags, precision=HIGH).astype(jnp.bfloat16)
    kim = jnp.einsum("qt,tkhij->qhkij", fwd_im, klags, precision=HIGH).astype(jnp.bfloat16)
    kspec = jnp.stack([kre, kim], 2).reshape(ntm, 2, nnz, block // (per_slot * ntm), block)
    kspec = lax.all_to_all(kspec, "tm", 0, 0, tiled=True)
    local_rows = pattern[:, 0] - my_state * rows_local
    kk = jnp.transpose(kspec, (2, 1, 0, 3, 4)).reshape(nnz, block, block)
    row_of = jnp.clip(local_rows, 0, rows_local - 1)
    real_slot = (my_slot != 0).astype(jnp.float32)

    col_block = pattern[:, 1]
    blocks_half = rows_local // per_slot
    rel = (col_block // rows_local - my_state) % nst
    rel = jnp.where(rel < nst // 2, rel, rel - nst)
    position = jnp.where(rel > 0, 2 * rel, -2 * rel - 1)
    position = jnp.where(rel == 0, 0, position)
    cb_half = (col_block // blocks_half) % per_slot
    cb_src = (cb_half != my_half).astype(jnp.int32)
    pick = position * blocks_half + col_block % blocks_half
    fwd = [(i, (i + 1) % nst) for i in range(nst)]
    bwd = [(i, (i - 1) % nst) for i in range(nst)]

    def ring_gather(x, kk):
        parts = [x]
        a = x
        b = x
        for step in range(1, nst // 2 + 1):
            if step == nst // 2:
                a, kk = lax.optimization_barrier((a, kk))
            a = lax.ppermute(a, "state", fwd)
            parts.append(a)
            if step < nst // 2:
                b = lax.ppermute(b, "state", bwd)
                parts.append(b)
        return jnp.stack(parts, 0), kk

    def respond(left, kk):
        xre = jnp.einsum("qt,tcn->qcn", fwd_re, left, precision=HIGH).astype(jnp.bfloat16)
        xim = jnp.einsum("qt,tcn->qcn", fwd_im, left, precision=HIGH).astype(jnp.bfloat16)
        xs = jnp.stack([xre, xim], 0).reshape(2, half, csl, per_slot, sh)
        xs = jnp.transpose(xs, (1, 3, 0, 2, 4)).reshape(ntm, 2, csl, sh)
        xs = lax.all_to_all(xs, "tm", 0, 0, tiled=True)
        xs = xs.reshape(ntm, 2, csl, blocks_half, block)
        xs = jnp.transpose(xs, (3, 1, 0, 2, 4)).reshape(blocks_half, 2, cols, block)
        mine, kk = ring_gather(xs, kk)
        other = lax.ppermute(mine, "tm", swap)
        mine = mine.reshape(nst * blocks_half, 2 * cols, block)
        other = other.reshape(nst * blocks_half, 2 * cols, block)
        prod = block_products(pick, cb_src, row_of, mine, other, kk, rows_local)
        ah = block // per_slot
        a, c_ = prod[:, :cols, :ah], prod[:, :cols, ah:]
        d, b = prod[:, cols:, :ah], prod[:, cols:, ah:]
        ys_re = a - real_slot * b
        ys_im = real_slot * (c_ + d) + (1.0 - real_slot) * b
        ys_re = jnp.transpose(ys_re, (1, 0, 2)).reshape(cols, rows_local * ah)
        ys_im = jnp.transpose(ys_im, (1, 0, 2)).reshape(cols, rows_local * ah)
        ys = jnp.stack([ys_re, ys_im], 0).reshape(2, ntm, csl, rows_local, block // per_slot)
        ys = jnp.transpose(ys, (1, 0, 2, 3, 4))
        ys = lax.all_to_all(ys, "tm", 0, 0, tiled=True)
        ys = ys.reshape(half, per_slot, 2, csl, rows_local, block // per_slot)
        ys = jnp.transpose(ys, (2, 0, 3, 4, 1, 5)).reshape(2, half, csl, states_local)
        return kk, jnp.einsum("tq,qcn->tcn", inv_re, ys[0], precision=HIGH) + jnp.einsum(
            "tq,qcn->tcn", inv_im, ys[1], precision=HIGH
        )

    field = solution[0].reshape(ntm, csl, states_local)
    field = lax.all_to_all(field, "tm", 0, 0, tiled=True)
    times = jnp.arange(length, dtype=jnp.int32)[:, None, None]
    for level_index in range(LEVELS):
        boundary = offsets[level_index]
        left = jnp.where(times < boundary, field, 0.0)
        kk, response = respond(left, kk)
        field = field + jnp.where(times >= boundary, response, 0.0)
    field = lax.all_to_all(field, "tm", 0, 0, tiled=True)
    return field.reshape(1, cols, states_local)


def solution(mesh):
    return jax.shard_map(
        shards,
        mesh=mesh,
        in_specs=(P("tm", None, "state"), P("state", "tm", None, None), P("state", None), P()),
        out_specs=P("tm", None, "state"),
        check_vma=False,
    )
```

```python
import math

import jax
import jax.numpy as jnp
import numpy as np
from jax import lax
from jax.experimental import pallas as pl
from jax.experimental.pallas import tpu as pltpu
from jax.sharding import PartitionSpec as P

LEVELS = 2
HIGH = lax.Precision.HIGHEST


def slot_tables(length):
    half = length // 2
    t = np.arange(length)
    q = np.arange(half)
    angle = 2.0 * np.pi * np.outer(q, t) / length
    fwd_re = np.cos(angle)
    fwd_im = -np.sin(angle)
    fwd_re[0] = 1.0
    fwd_im[0] = np.cos(np.pi * t)
    inv_re = 2.0 * np.cos(angle.T) / length
    inv_im = -2.0 * np.sin(angle.T) / length
    inv_re[:, 0] = 1.0 / length
    inv_im[:, 0] = np.cos(np.pi * t) / length
    return tuple(jnp.asarray(a, jnp.float32) for a in (fwd_re, fwd_im, inv_re, inv_im))


def _products_body(pick_ref, src_ref, row_ref, mine_ref, other_ref, kk_ref, out_ref):
    out_ref[...] = jnp.zeros_like(out_ref)

    def step(k, carry):
        p = pick_ref[k]
        x = jnp.where(src_ref[k] == 1, other_ref[p], mine_ref[p])
        prod = lax.dot_general(
            x, kk_ref[k], (((1,), (1,)), ((), ())), preferred_element_type=jnp.float32
        )
        r = row_ref[k]
        out_ref[r] = out_ref[r] + prod
        return carry

    lax.fori_loop(0, kk_ref.shape[0], step, 0, unroll=8)


def block_products(pick, src, row, mine, other, kk, rows_local):
    nblk, m, j = mine.shape
    nnz, n, _ = kk.shape
    full = lambda *shape: pl.BlockSpec(shape, lambda i, *_: (0,) * len(shape))
    return pl.pallas_call(
        _products_body,
        grid_spec=pltpu.PrefetchScalarGridSpec(
            num_scalar_prefetch=3,
            grid=(1,),
            in_specs=[full(nblk, m, j), full(nblk, m, j), full(nnz, n, j)],
            out_specs=full(rows_local, m, n),
        ),
        out_shape=jax.ShapeDtypeStruct((rows_local, m, n), jnp.float32),
    )(pick, src, row, mine, other, kk)


def shards(solution, kernel, pattern, offsets):
    ntm = lax.axis_size("tm")
    nst = lax.axis_size("state")
    length = solution.shape[0] * ntm
    half = length // 2
    per_slot = ntm // half
    cols = solution.shape[1]
    states_local = solution.shape[2]
    nnz, _, block, _ = kernel.shape
    rows_local = states_local // block
    csl = cols // ntm
    sh = states_local // per_slot
    fwd_re, fwd_im, inv_re, inv_im = slot_tables(length)

    me = lax.axis_index("tm")
    my_state = lax.axis_index("state")
    my_slot = me // per_slot
    my_half = me % per_slot
    swap = [(i, i ^ 1) for i in range(ntm)]

    ksrc = kernel[:, 0].reshape(nnz, per_slot, ntm, block // (per_slot * ntm), block)
    ksrc = jnp.transpose(ksrc, (2, 0, 1, 3, 4))
    klags = lax.all_to_all(ksrc, "tm", 0, 0, tiled=True).astype(jnp.float32)
    kre = jnp.einsum("qt,tkhij->qhkij", fwd_re, klags, precision=HIGH).astype(jnp.bfloat16)
    kim = jnp.einsum("qt,tkhij->qhkij", fwd_im, klags, precision=HIGH).astype(jnp.bfloat16)
    kspec = jnp.stack([kre, kim], 2).reshape(ntm, 2, nnz, block // (per_slot * ntm), block)
    kspec = lax.all_to_all(kspec, "tm", 0, 0, tiled=True)
    local_rows = pattern[:, 0] - my_state * rows_local
    kk = jnp.transpose(kspec, (2, 1, 0, 3, 4)).reshape(nnz, block, block)
    row_of = jnp.clip(local_rows, 0, rows_local - 1)
    real_slot = (my_slot != 0).astype(jnp.float32)

    col_block = pattern[:, 1]
    blocks_half = rows_local // per_slot
    rel = (col_block // rows_local - my_state) % nst
    rel = jnp.where(rel < nst // 2, rel, rel - nst)
    position = jnp.where(rel > 0, 2 * rel, -2 * rel - 1)
    position = jnp.where(rel == 0, 0, position)
    cb_half = (col_block // blocks_half) % per_slot
    cb_src = (cb_half != my_half).astype(jnp.int32)
    pick = position * blocks_half + col_block % blocks_half
    fwd = [(i, (i + 1) % nst) for i in range(nst)]
    bwd = [(i, (i - 1) % nst) for i in range(nst)]

    def ring_gather(x):
        parts = [x]
        a = x
        b = x
        for step in range(1, nst // 2 + 1):
            a = lax.ppermute(a, "state", fwd)
            parts.append(a)
            if step < nst // 2:
                b = lax.ppermute(b, "state", bwd)
                parts.append(b)
        return jnp.concatenate(parts, 0)

    def respond(left):
        xre = jnp.einsum("qt,tcn->qcn", fwd_re, left, precision=HIGH).astype(jnp.bfloat16)
        xim = jnp.einsum("qt,tcn->qcn", fwd_im, left, precision=HIGH).astype(jnp.bfloat16)
        xs = jnp.stack([xre, xim], 0).reshape(2, half, csl, per_slot, sh)
        xs = jnp.transpose(xs, (1, 3, 0, 2, 4)).reshape(ntm, 2, csl, sh)
        xs = lax.all_to_all(xs, "tm", 0, 0, tiled=True)
        xs = xs.reshape(ntm, 2, csl, blocks_half, block)
        xs = jnp.transpose(xs, (3, 1, 0, 2, 4)).reshape(blocks_half, 2 * cols, block)
        mine = ring_gather(xs)
        other = lax.ppermute(mine, "tm", swap)
        prod = block_products(pick, cb_src, row_of, mine, other, kk, rows_local)
        ah = block // per_slot
        a, c_ = prod[:, :cols, :ah], prod[:, :cols, ah:]
        d, b = prod[:, cols:, :ah], prod[:, cols:, ah:]
        ys_re = a - real_slot * b
        ys_im = real_slot * (c_ + d) + (1.0 - real_slot) * b
        ys_re = jnp.transpose(ys_re, (1, 0, 2)).reshape(cols, rows_local * ah)
        ys_im = jnp.transpose(ys_im, (1, 0, 2)).reshape(cols, rows_local * ah)
        ys = jnp.stack([ys_re, ys_im], 0).reshape(2, ntm, csl, rows_local, block // per_slot)
        ys = jnp.transpose(ys, (1, 0, 2, 3, 4))
        ys = lax.all_to_all(ys, "tm", 0, 0, tiled=True)
        ys = ys.reshape(half, per_slot, 2, csl, rows_local, block // per_slot)
        ys = jnp.transpose(ys, (2, 0, 3, 4, 1, 5)).reshape(2, half, csl, states_local)
        return jnp.einsum("tq,qcn->tcn", inv_re, ys[0], precision=HIGH) + jnp.einsum(
            "tq,qcn->tcn", inv_im, ys[1], precision=HIGH
        )

    field = solution[0].reshape(ntm, csl, states_local)
    field = lax.all_to_all(field, "tm", 0, 0, tiled=True)
    times = jnp.arange(length, dtype=jnp.int32)[:, None, None]
    for level_index in range(LEVELS):
        boundary = offsets[level_index]
        left = jnp.where(times < boundary, field, 0.0)
        response = respond(left)
        field = field + jnp.where(times >= boundary, response, 0.0)
    field = lax.all_to_all(field, "tm", 0, 0, tiled=True)
    return field.reshape(1, cols, states_local)


def solution(mesh):
    return jax.shard_map(
        shards,
        mesh=mesh,
        in_specs=(P("tm", None, "state"), P("state", "tm", None, None), P("state", None), P()),
        out_specs=P("tm", None, "state"),
        check_vma=False,
    )
```

```python
import math

import jax
import jax.numpy as jnp
import numpy as np
from jax import lax
from jax.experimental import pallas as pl
from jax.experimental.pallas import tpu as pltpu
from jax.sharding import PartitionSpec as P

LEVELS = 2
HIGH = lax.Precision.HIGHEST


def slot_tables(length):
    half = length // 2
    t = np.arange(length)
    q = np.arange(half)
    angle = 2.0 * np.pi * np.outer(q, t) / length
    fwd_re = np.cos(angle)
    fwd_im = -np.sin(angle)
    fwd_re[0] = 1.0
    fwd_im[0] = np.cos(np.pi * t)
    inv_re = 2.0 * np.cos(angle.T) / length
    inv_im = -2.0 * np.sin(angle.T) / length
    inv_re[:, 0] = 1.0 / length
    inv_im[:, 0] = np.cos(np.pi * t) / length
    fwd = np.concatenate([fwd_re, fwd_im], 0)
    inv = np.concatenate([inv_re, inv_im], 1)
    return jnp.asarray(fwd, jnp.float32), jnp.asarray(inv, jnp.float32)


def _products_body(pick_ref, src_ref, row_ref, mine_ref, other_ref, kk_ref, out_ref):
    out_ref[...] = jnp.zeros_like(out_ref)

    def step(k, carry):
        p = pick_ref[k]
        x = jnp.where(src_ref[k] == 1, other_ref[p], mine_ref[p])
        prod = lax.dot_general(
            x, kk_ref[k], (((1,), (1,)), ((), ())), preferred_element_type=jnp.float32
        )
        r = row_ref[k]
        out_ref[r] = out_ref[r] + prod
        return carry

    lax.fori_loop(0, kk_ref.shape[0], step, 0, unroll=8)


def block_products(pick, src, row, mine, other, kk, rows_local):
    nblk, m, j = mine.shape
    nnz, n, _ = kk.shape
    full = lambda *shape: pl.BlockSpec(shape, lambda i, *_: (0,) * len(shape))
    return pl.pallas_call(
        _products_body,
        grid_spec=pltpu.PrefetchScalarGridSpec(
            num_scalar_prefetch=3,
            grid=(1,),
            in_specs=[full(nblk, m, j), full(nblk, m, j), full(nnz, n, j)],
            out_specs=full(rows_local, m, n),
        ),
        out_shape=jax.ShapeDtypeStruct((rows_local, m, n), jnp.float32),
    )(pick, src, row, mine, other, kk)


def shards(solution, kernel, pattern, offsets):
    ntm = lax.axis_size("tm")
    nst = lax.axis_size("state")
    length = solution.shape[0] * ntm
    half = length // 2
    per_slot = ntm // half
    cols = solution.shape[1]
    states_local = solution.shape[2]
    nnz, _, block, _ = kernel.shape
    rows_local = states_local // block
    csl = cols // ntm
    sh = states_local // per_slot
    fwd_table, inv_table = slot_tables(length)

    me = lax.axis_index("tm")
    my_state = lax.axis_index("state")
    my_slot = me // per_slot
    my_half = me % per_slot
    swap = [(i, i ^ 1) for i in range(ntm)]

    ksrc = kernel[:, 0].reshape(nnz, per_slot, ntm, block // (per_slot * ntm), block)
    ksrc = jnp.transpose(ksrc, (2, 0, 1, 3, 4))
    klags = lax.all_to_all(ksrc, "tm", 0, 0, tiled=True).astype(jnp.float32)
    kspec = jnp.einsum(
        "xqt,tkhij->qhxkij", fwd_table.reshape(2, half, length), klags, precision=HIGH
    ).astype(jnp.bfloat16)
    kspec = kspec.reshape(ntm, 2, nnz, block // (per_slot * ntm), block)
    kspec = lax.all_to_all(kspec, "tm", 0, 0, tiled=True)
    local_rows = pattern[:, 0] - my_state * rows_local
    kk = jnp.transpose(kspec, (2, 1, 0, 3, 4)).reshape(nnz, block, block)
    row_of = jnp.clip(local_rows, 0, rows_local - 1)
    real_slot = (my_slot != 0).astype(jnp.float32)

    col_block = pattern[:, 1]
    blocks_half = rows_local // per_slot
    rel = (col_block // rows_local - my_state) % nst
    rel = jnp.where(rel < nst // 2, rel, rel - nst)
    position = jnp.where(rel > 0, 2 * rel, -2 * rel - 1)
    position = jnp.where(rel == 0, 0, position)
    cb_half = (col_block // blocks_half) % per_slot
    cb_src = (cb_half != my_half).astype(jnp.int32)
    pick = position * blocks_half + col_block % blocks_half
    fwd = [(i, (i + 1) % nst) for i in range(nst)]
    bwd = [(i, (i - 1) % nst) for i in range(nst)]

    def ring_gather(x):
        parts = [x]
        a = x
        b = x
        for step in range(1, nst // 2 + 1):
            a = lax.ppermute(a, "state", fwd)
            parts.append(a)
            if step < nst // 2:
                b = lax.ppermute(b, "state", bwd)
                parts.append(b)
        return jnp.concatenate(parts, 0)

    def respond(left):
        xs = jnp.einsum("qt,tcn->qcn", fwd_table, left, precision=HIGH).astype(jnp.bfloat16)
        xs = xs.reshape(2, half, csl, per_slot, sh)
        xs = jnp.transpose(xs, (1, 3, 0, 2, 4)).reshape(ntm, 2, csl, sh)
        xs = lax.all_to_all(xs, "tm", 0, 0, tiled=True)
        xs = xs.reshape(ntm, 2, csl, blocks_half, block)
        xs = jnp.transpose(xs, (3, 1, 0, 2, 4)).reshape(blocks_half, 2 * cols, block)
        mine = ring_gather(xs)
        other = lax.ppermute(mine, "tm", swap)
        prod = block_products(pick, cb_src, row_of, mine, other, kk, rows_local)
        ah = block // per_slot
        a, c_ = prod[:, :cols, :ah], prod[:, :cols, ah:]
        d, b = prod[:, cols:, :ah], prod[:, cols:, ah:]
        ys_re = a - real_slot * b
        ys_im = real_slot * (c_ + d) + (1.0 - real_slot) * b
        ys_re = jnp.transpose(ys_re, (1, 0, 2)).reshape(cols, rows_local * ah)
        ys_im = jnp.transpose(ys_im, (1, 0, 2)).reshape(cols, rows_local * ah)
        ys = jnp.stack([ys_re, ys_im], 0).reshape(2, ntm, csl, rows_local, block // per_slot)
        ys = jnp.transpose(ys, (1, 0, 2, 3, 4))
        ys = lax.all_to_all(ys, "tm", 0, 0, tiled=True)
        ys = ys.reshape(half, per_slot, 2, csl, rows_local, block // per_slot)
        ys = jnp.transpose(ys, (2, 0, 3, 4, 1, 5)).reshape(2, half, csl, states_local)
        return jnp.einsum("tq,qcn->tcn", inv_table, ys.reshape(length, csl, states_local), precision=HIGH)

    field = solution[0].reshape(ntm, csl, states_local)
    field = lax.all_to_all(field, "tm", 0, 0, tiled=True)
    times = jnp.arange(length, dtype=jnp.int32)[:, None, None]
    for level_index in range(LEVELS):
        boundary = offsets[level_index]
        left = jnp.where(times < boundary, field, 0.0)
        response = respond(left)
        field = field + jnp.where(times >= boundary, response, 0.0)
    field = lax.all_to_all(field, "tm", 0, 0, tiled=True)
    return field.reshape(1, cols, states_local)


def solution(mesh):
    return jax.shard_map(
        shards,
        mesh=mesh,
        in_specs=(P("tm", None, "state"), P("state", "tm", None, None), P("state", None), P()),
        out_specs=P("tm", None, "state"),
        check_vma=False,
    )
```

```python
import jax
import jax.numpy as jnp
import numpy as np
from jax import lax
from jax.experimental import pallas as pl
from jax.experimental.pallas import tpu as pltpu
from jax.sharding import PartitionSpec as P


LEVELS = 2
HIGH = lax.Precision.HIGHEST


def slot_tables(length):
    half = length // 2
    t = np.arange(length)
    q = np.arange(half)
    angle = 2.0 * np.pi * np.outer(q, t) / length
    fwd_re = np.cos(angle)
    fwd_im = -np.sin(angle)
    fwd_re[0] = 1.0
    fwd_im[0] = np.cos(np.pi * t)
    inv_re = 2.0 * np.cos(angle.T) / length
    inv_im = -2.0 * np.sin(angle.T) / length
    inv_re[:, 0] = 1.0 / length
    inv_im[:, 0] = np.cos(np.pi * t) / length
    fwd = np.concatenate([fwd_re, fwd_im], 0)
    inv = np.concatenate([inv_re, inv_im], 1)
    return jnp.asarray(fwd, jnp.float32), jnp.asarray(inv, jnp.float32)


def _products_body(pick_ref, src_ref, row_ref, mine_ref, other_ref, kk_ref, out_ref):
    out_ref[...] = jnp.zeros_like(out_ref)

    def step(k, carry):
        p = pick_ref[k]
        x = jnp.where(src_ref[k] == 1, other_ref[p], mine_ref[p])
        prod = lax.dot_general(
            x, kk_ref[k], (((1,), (1,)), ((), ())), preferred_element_type=jnp.float32
        )
        r = row_ref[k]
        out_ref[r] = out_ref[r] + prod
        return carry

    lax.fori_loop(0, kk_ref.shape[0], step, 0, unroll=8)


def block_products(pick, src, row, mine, other, kk, rows_local):
    nblk, m, j = mine.shape
    nnz, n, _ = kk.shape
    full = lambda *shape: pl.BlockSpec(shape, lambda i, *_: (0,) * len(shape))
    return pl.pallas_call(
        _products_body,
        grid_spec=pltpu.PrefetchScalarGridSpec(
            num_scalar_prefetch=3,
            grid=(1,),
            in_specs=[full(nblk, m, j), full(nblk, m, j), full(nnz, n, j)],
            out_specs=full(rows_local, m, n),
        ),
        out_shape=jax.ShapeDtypeStruct((rows_local, m, n), jnp.float32),
    )(pick, src, row, mine, other, kk)


def shards(solution, kernel, pattern, offsets):
    ntm = lax.axis_size("tm")
    nst = lax.axis_size("state")
    length = solution.shape[0] * ntm
    half = length // 2
    per_slot = ntm // half
    cols = solution.shape[1]
    states_local = solution.shape[2]
    nnz, _, block, _ = kernel.shape
    rows_local = states_local // block
    csl = cols // ntm
    sh = states_local // per_slot
    fwd_table, inv_table = slot_tables(length)

    me = lax.axis_index("tm")
    my_state = lax.axis_index("state")
    my_slot = me // per_slot
    my_half = me % per_slot
    swap = [(i, i ^ 1) for i in range(ntm)]

    ksrc = kernel[:, 0].reshape(nnz, per_slot, ntm, block // (per_slot * ntm), block)
    ksrc = jnp.transpose(ksrc, (2, 0, 1, 3, 4))
    klags = lax.all_to_all(ksrc, "tm", 0, 0, tiled=True).astype(jnp.float32)

    def kernel_spectrum():
        kspec = jnp.einsum(
            "xqt,tkhij->qhxkij", fwd_table.reshape(2, half, length), klags, precision=HIGH
        ).astype(jnp.bfloat16)
        kspec = kspec.reshape(ntm, 2, nnz, block // (per_slot * ntm), block)
        kspec = lax.all_to_all(kspec, "tm", 0, 0, tiled=True)
        return jnp.transpose(kspec, (2, 1, 0, 3, 4)).reshape(nnz, block, block)

    local_rows = pattern[:, 0] - my_state * rows_local
    row_of = jnp.clip(local_rows, 0, rows_local - 1)
    real_slot = (my_slot != 0).astype(jnp.float32)

    col_block = pattern[:, 1]
    blocks_half = rows_local // per_slot
    rel = (col_block // rows_local - my_state) % nst
    rel = jnp.where(rel < nst // 2, rel, rel - nst)
    position = jnp.where(rel > 0, 2 * rel, -2 * rel - 1)
    position = jnp.where(rel == 0, 0, position)
    cb_half = (col_block // blocks_half) % per_slot
    cb_src = (cb_half != my_half).astype(jnp.int32)
    pick_ring = position * blocks_half + col_block % blocks_half
    pick_ordered = (col_block // rows_local) * blocks_half + col_block % blocks_half
    fwd = [(i, (i + 1) % nst) for i in range(nst)]
    bwd = [(i, (i - 1) % nst) for i in range(nst)]

    def ring_gather(x):
        parts = [x]
        a = x
        b = x
        for step in range(1, nst // 2 + 1):
            a = lax.ppermute(a, "state", fwd)
            parts.append(a)
            if step < nst // 2:
                b = lax.ppermute(b, "state", bwd)
                parts.append(b)
        return jnp.concatenate(parts, 0)

    def respond(left, on_ring):
        xs = jnp.einsum("qt,tcn->qcn", fwd_table, left, precision=HIGH).astype(jnp.bfloat16)
        xs = xs.reshape(2, half, csl, per_slot, sh)
        xs = jnp.transpose(xs, (1, 3, 0, 2, 4)).reshape(ntm, 2, csl, sh)
        xs = lax.all_to_all(xs, "tm", 0, 0, tiled=True)
        xs = xs.reshape(ntm, 2, csl, blocks_half, block)
        xs = jnp.transpose(xs, (3, 1, 0, 2, 4)).reshape(blocks_half, 2 * cols, block)
        if on_ring:
            mine = ring_gather(xs)
            pick = pick_ring
            kk = kk_prev
        else:
            mine = lax.all_gather(xs, "state", axis=0, tiled=True)
            pick = pick_ordered
            kk = kernel_spectrum()
        other = lax.ppermute(mine, "tm", swap)
        prod = block_products(pick, cb_src, row_of, mine, other, kk, rows_local)
        ah = block // per_slot
        a, c_ = prod[:, :cols, :ah], prod[:, :cols, ah:]
        d, b = prod[:, cols:, :ah], prod[:, cols:, ah:]
        ys_re = a - real_slot * b
        ys_im = real_slot * (c_ + d) + (1.0 - real_slot) * b
        ys_re = jnp.transpose(ys_re, (1, 0, 2)).reshape(cols, rows_local * ah)
        ys_im = jnp.transpose(ys_im, (1, 0, 2)).reshape(cols, rows_local * ah)
        ys = jnp.stack([ys_re, ys_im], 0).reshape(2, ntm, csl, rows_local, block // per_slot)
        ys = jnp.transpose(ys, (1, 0, 2, 3, 4))
        ys = lax.all_to_all(ys, "tm", 0, 0, tiled=True)
        ys = ys.reshape(half, per_slot, 2, csl, rows_local, block // per_slot)
        ys = jnp.transpose(ys, (2, 0, 3, 4, 1, 5)).reshape(2, half, csl, states_local)
        return kk, jnp.einsum("tq,qcn->tcn", inv_table, ys.reshape(length, csl, states_local), precision=HIGH)

    field = solution[0].reshape(ntm, csl, states_local)
    field = lax.all_to_all(field, "tm", 0, 0, tiled=True)
    times = jnp.arange(length, dtype=jnp.int32)[:, None, None]
    kk_prev = None
    for level_index in range(LEVELS):
        boundary = offsets[level_index]
        left = jnp.where(times < boundary, field, 0.0)
        kk_prev, response = respond(left, level_index > 0)
        field = field + jnp.where(times >= boundary, response, 0.0)
    field = lax.all_to_all(field, "tm", 0, 0, tiled=True)
    return field.reshape(1, cols, states_local)


def solution(mesh):
    return jax.shard_map(
        shards,
        mesh=mesh,
        in_specs=(P("tm", None, "state"), P("state", "tm", None, None), P("state", None), P()),
        out_specs=P("tm", None, "state"),
        check_vma=False,
    )
```

```python
import math

import jax
import jax.numpy as jnp
import numpy as np
from jax import lax
from jax.experimental import pallas as pl
from jax.experimental.pallas import tpu as pltpu
from jax.sharding import PartitionSpec as P

LEVELS = 2
HIGH = lax.Precision.HIGHEST


def slot_tables(length):
    half = length // 2
    t = np.arange(length)
    q = np.arange(half)
    angle = 2.0 * np.pi * np.outer(q, t) / length
    fwd_re = np.cos(angle)
    fwd_im = -np.sin(angle)
    fwd_re[0] = 1.0
    fwd_im[0] = np.cos(np.pi * t)
    inv_re = 2.0 * np.cos(angle.T) / length
    inv_im = -2.0 * np.sin(angle.T) / length
    inv_re[:, 0] = 1.0 / length
    inv_im[:, 0] = np.cos(np.pi * t) / length
    fwd = np.concatenate([fwd_re, fwd_im], 0)
    inv = np.concatenate([inv_re, inv_im], 1)
    return jnp.asarray(fwd, jnp.float32), jnp.asarray(inv, jnp.float32)


def _products_body(pick_ref, src_ref, row_ref, mine_ref, other_ref, kk_ref, out_ref):
    out_ref[...] = jnp.zeros_like(out_ref)

    def step(k, carry):
        p = pick_ref[k]
        x = jnp.where(src_ref[k] == 1, other_ref[p], mine_ref[p])
        prod = lax.dot_general(
            x, kk_ref[k], (((1,), (1,)), ((), ())), preferred_element_type=jnp.float32
        )
        r = row_ref[k]
        out_ref[r] = out_ref[r] + prod
        return carry

    lax.fori_loop(0, kk_ref.shape[0], step, 0, unroll=8)


def block_products(pick, src, row, mine, other, kk, rows_local):
    nblk, m, j = mine.shape
    nnz, n, _ = kk.shape
    full = lambda *shape: pl.BlockSpec(shape, lambda i, *_: (0,) * len(shape))
    return pl.pallas_call(
        _products_body,
        grid_spec=pltpu.PrefetchScalarGridSpec(
            num_scalar_prefetch=3,
            grid=(1,),
            in_specs=[full(nblk, m, j), full(nblk, m, j), full(nnz, n, j)],
            out_specs=full(rows_local, m, n),
        ),
        out_shape=jax.ShapeDtypeStruct((rows_local, m, n), jnp.float32),
    )(pick, src, row, mine, other, kk)


def shards(solution, kernel, pattern, offsets):
    ntm = lax.axis_size("tm")
    nst = lax.axis_size("state")
    length = solution.shape[0] * ntm
    half = length // 2
    per_slot = ntm // half
    cols = solution.shape[1]
    states_local = solution.shape[2]
    nnz, _, block, _ = kernel.shape
    rows_local = states_local // block
    csl = cols // ntm
    sh = states_local // per_slot
    fwd_table, inv_table = slot_tables(length)

    me = lax.axis_index("tm")
    my_state = lax.axis_index("state")
    my_slot = me // per_slot
    my_half = me % per_slot
    swap = [(i, i ^ 1) for i in range(ntm)]

    ksrc = kernel[:, 0].reshape(nnz, per_slot, ntm, block // (per_slot * ntm), block)
    ksrc = jnp.transpose(ksrc, (2, 0, 1, 3, 4))
    klags = lax.all_to_all(ksrc, "tm", 0, 0, tiled=True).astype(jnp.float32)
    kspec = jnp.einsum(
        "xqt,tkhij->qhxkij", fwd_table.reshape(2, half, length), klags, precision=HIGH
    ).astype(jnp.bfloat16)
    kspec = kspec.reshape(ntm, 2, nnz, block // (per_slot * ntm), block)
    kspec = lax.all_to_all(kspec, "tm", 0, 0, tiled=True)
    local_rows = pattern[:, 0] - my_state * rows_local
    kk = jnp.transpose(kspec, (2, 1, 0, 3, 4)).reshape(nnz, block, block)
    row_of = jnp.clip(local_rows, 0, rows_local - 1)
    real_slot = (my_slot != 0).astype(jnp.float32)

    col_block = pattern[:, 1]
    blocks_half = rows_local // per_slot
    rel = (col_block // rows_local - my_state) % nst
    rel = jnp.where(rel < nst // 2, rel, rel - nst)
    position = jnp.where(rel > 0, 2 * rel, -2 * rel - 1)
    position = jnp.where(rel == 0, 0, position)
    cb_half = (col_block // blocks_half) % per_slot
    cb_src = (cb_half != my_half).astype(jnp.int32)
    pick = position * blocks_half + col_block % blocks_half
    fwd = [(i, (i + 1) % nst) for i in range(nst)]
    bwd = [(i, (i - 1) % nst) for i in range(nst)]

    def ring_gather(x):
        parts = [x]
        a = x
        b = x
        for step in range(1, nst // 2 + 1):
            a = lax.ppermute(a, "state", fwd)
            parts.append(a)
            if step < nst // 2:
                b = lax.ppermute(b, "state", bwd)
                parts.append(b)
        return jnp.concatenate(parts, 0)

    def respond(left):
        xs = jnp.einsum("qt,tcn->qcn", fwd_table, left, precision=HIGH).astype(jnp.bfloat16)
        xs = xs.reshape(2, half, csl, per_slot, sh)
        xs = jnp.transpose(xs, (1, 3, 0, 2, 4)).reshape(ntm, 2, csl, sh)
        xs = lax.all_to_all(xs, "tm", 0, 0, tiled=True)
        xs = xs.reshape(ntm, 2, csl, blocks_half, block)
        xs = jnp.transpose(xs, (3, 1, 0, 2, 4)).reshape(blocks_half, 2 * cols, block)
        mine = ring_gather(xs)
        other = lax.ppermute(mine, "tm", swap)
        prod = block_products(pick, cb_src, row_of, mine, other, kk, rows_local)
        ah = block // per_slot
        a, c_ = prod[:, :cols, :ah], prod[:, :cols, ah:]
        d, b = prod[:, cols:, :ah], prod[:, cols:, ah:]
        ys_re = a - real_slot * b
        ys_im = real_slot * (c_ + d) + (1.0 - real_slot) * b
        ys = jnp.stack([ys_re, ys_im], 0).reshape(2, rows_local, ntm, csl, ah)
        ys = jnp.transpose(ys, (2, 0, 3, 1, 4)).reshape(ntm, -1, 2 * ah)
        ys = lax.all_to_all(ys, "tm", 0, 0, tiled=True)
        ys = ys.reshape(half, per_slot, 2, csl, rows_local // 2, 2, ah)
        ys = jnp.transpose(ys, (2, 0, 3, 4, 5, 1, 6)).reshape(2, half, csl, states_local)
        return jnp.einsum("tq,qcn->tcn", inv_table, ys.reshape(length, csl, states_local), precision=HIGH)

    field = solution[0].reshape(ntm, csl, states_local)
    field = lax.all_to_all(field, "tm", 0, 0, tiled=True)
    times = jnp.arange(length, dtype=jnp.int32)[:, None, None]
    for level_index in range(LEVELS):
        boundary = offsets[level_index]
        left = jnp.where(times < boundary, field, 0.0)
        response = respond(left)
        field = field + jnp.where(times >= boundary, response, 0.0)
    field = lax.all_to_all(field, "tm", 0, 0, tiled=True)
    return field.reshape(1, cols, states_local)


def solution(mesh):
    return jax.shard_map(
        shards,
        mesh=mesh,
        in_specs=(P("tm", None, "state"), P("state", "tm", None, None), P("state", None), P()),
        out_specs=P("tm", None, "state"),
        check_vma=False,
    )
```

```python
import math

import jax
import jax.numpy as jnp
import numpy as np
from jax import lax
from jax.experimental import pallas as pl
from jax.experimental.pallas import tpu as pltpu
from jax.sharding import PartitionSpec as P

LEVELS = 2
HIGH = lax.Precision.HIGHEST


def slot_tables(length):
    half = length // 2
    t = np.arange(length)
    q = np.arange(half)
    angle = 2.0 * np.pi * np.outer(q, t) / length
    fwd_re = np.cos(angle)
    fwd_im = -np.sin(angle)
    fwd_re[0] = 1.0
    fwd_im[0] = np.cos(np.pi * t)
    inv_re = 2.0 * np.cos(angle.T) / length
    inv_im = -2.0 * np.sin(angle.T) / length
    inv_re[:, 0] = 1.0 / length
    inv_im[:, 0] = np.cos(np.pi * t) / length
    fwd = np.concatenate([fwd_re, fwd_im], 0)
    inv = np.concatenate([inv_re, inv_im], 1)
    return jnp.asarray(fwd, jnp.float32), jnp.asarray(inv, jnp.float32)


def _products_body(pick_ref, src_ref, row_ref, mine_ref, other_ref, kk_ref, out_ref):
    out_ref[...] = jnp.zeros_like(out_ref)

    def step(k, carry):
        p = pick_ref[k]
        x = jnp.where(src_ref[k] == 1, other_ref[p], mine_ref[p])
        prod = lax.dot_general(
            x, kk_ref[k], (((1,), (1,)), ((), ())), preferred_element_type=jnp.float32
        )
        r = row_ref[k]
        out_ref[r] = out_ref[r] + prod
        return carry

    lax.fori_loop(0, kk_ref.shape[0], step, 0, unroll=8)


def block_products(pick, src, row, mine, other, kk, rows_local):
    nblk, m, j = mine.shape
    nnz, n, _ = kk.shape
    full = lambda *shape: pl.BlockSpec(shape, lambda i, *_: (0,) * len(shape))
    return pl.pallas_call(
        _products_body,
        grid_spec=pltpu.PrefetchScalarGridSpec(
            num_scalar_prefetch=3,
            grid=(1,),
            in_specs=[full(nblk, m, j), full(nblk, m, j), full(nnz, n, j)],
            out_specs=full(rows_local, m, n),
        ),
        out_shape=jax.ShapeDtypeStruct((rows_local, m, n), jnp.float32),
    )(pick, src, row, mine, other, kk)


def shards(solution, kernel, pattern, offsets):
    ntm = lax.axis_size("tm")
    nst = lax.axis_size("state")
    length = solution.shape[0] * ntm
    half = length // 2
    per_slot = ntm // half
    cols = solution.shape[1]
    states_local = solution.shape[2]
    nnz, _, block, _ = kernel.shape
    rows_local = states_local // block
    csl = cols // ntm
    sh = states_local // per_slot
    fwd_table, inv_table = slot_tables(length)

    me = lax.axis_index("tm")
    my_state = lax.axis_index("state")
    my_slot = me // per_slot
    my_half = me % per_slot
    swap = [(i, i ^ 1) for i in range(ntm)]

    ksrc = kernel[:, 0].reshape(nnz, per_slot, ntm, block // (per_slot * ntm), block)
    ksrc = jnp.transpose(ksrc, (2, 0, 1, 3, 4))
    klags = lax.all_to_all(ksrc, "tm", 0, 0, tiled=True).astype(jnp.float32)
    kspec = jnp.einsum(
        "xqt,tkhij->qhxkij", fwd_table.reshape(2, half, length), klags, precision=HIGH
    ).astype(jnp.bfloat16)
    kspec = kspec.reshape(ntm, 2, nnz, block // (per_slot * ntm), block)
    kspec = lax.all_to_all(kspec, "tm", 0, 0, tiled=True)
    local_rows = pattern[:, 0] - my_state * rows_local
    kk = jnp.transpose(kspec, (2, 1, 0, 3, 4)).reshape(nnz, block, block)
    row_of = jnp.clip(local_rows, 0, rows_local - 1)
    real_slot = (my_slot != 0).astype(jnp.float32)

    col_block = pattern[:, 1]
    blocks_half = rows_local // per_slot
    rel = (col_block // rows_local - my_state) % nst
    rel = jnp.where(rel < nst // 2, rel, rel - nst)
    position = jnp.where(rel > 0, 2 * rel, -2 * rel - 1)
    position = jnp.where(rel == 0, 0, position)
    cb_half = (col_block // blocks_half) % per_slot
    cb_src = (cb_half != my_half).astype(jnp.int32)
    pick = position * blocks_half + col_block % blocks_half
    fwd = [(i, (i + 1) % nst) for i in range(nst)]
    bwd = [(i, (i - 1) % nst) for i in range(nst)]

    def ring_gather(x):
        parts = [x]
        a = x
        b = x
        for step in range(1, nst // 2 + 1):
            a = lax.ppermute(a, "state", fwd)
            parts.append(a)
            if step < nst // 2:
                b = lax.ppermute(b, "state", bwd)
                parts.append(b)
        return jnp.concatenate(parts, 0)

    def respond(left):
        xs = jnp.einsum("qt,tcn->qcn", fwd_table, left, precision=HIGH).astype(jnp.bfloat16)
        xs = xs.reshape(2, half, csl, per_slot, blocks_half, block)
        xs = jnp.transpose(xs, (1, 3, 0, 2, 4, 5)).reshape(ntm, -1, block)
        xs = lax.all_to_all(xs, "tm", 0, 0, tiled=True)
        xs = xs.reshape(ntm, 2, csl, blocks_half, block)
        xs = jnp.transpose(xs, (3, 1, 0, 2, 4)).reshape(blocks_half, 2 * cols, block)
        mine = ring_gather(xs)
        other = lax.ppermute(mine, "tm", swap)
        prod = block_products(pick, cb_src, row_of, mine, other, kk, rows_local)
        ah = block // per_slot
        a, c_ = prod[:, :cols, :ah], prod[:, :cols, ah:]
        d, b = prod[:, cols:, :ah], prod[:, cols:, ah:]
        ys_re = a - real_slot * b
        ys_im = real_slot * (c_ + d) + (1.0 - real_slot) * b
        ys = jnp.stack([ys_re, ys_im], 0).reshape(2, rows_local, ntm, csl, ah)
        ys = jnp.transpose(ys, (2, 0, 3, 1, 4)).reshape(ntm, -1, 2 * ah)
        ys = lax.all_to_all(ys, "tm", 0, 0, tiled=True)
        ys = ys.reshape(half, per_slot, 2, csl, rows_local // 2, 2, ah)
        ys = jnp.transpose(ys, (2, 0, 3, 4, 5, 1, 6)).reshape(length, csl * rows_local, block)
        return jnp.einsum("tq,qcn->tcn", inv_table, ys, precision=HIGH)

    field = solution[0].reshape(ntm, csl * rows_local, block)
    field = lax.all_to_all(field, "tm", 0, 0, tiled=True)
    times = jnp.arange(length, dtype=jnp.int32)[:, None, None]
    for level_index in range(LEVELS):
        boundary = offsets[level_index]
        left = jnp.where(times < boundary, field, 0.0)
        response = respond(left)
        field = field + jnp.where(times >= boundary, response, 0.0)
    field = lax.all_to_all(field, "tm", 0, 0, tiled=True)
    return field.reshape(1, cols, states_local)


def solution(mesh):
    return jax.shard_map(
        shards,
        mesh=mesh,
        in_specs=(P("tm", None, "state"), P("state", "tm", None, None), P("state", None), P()),
        out_specs=P("tm", None, "state"),
        check_vma=False,
    )
```

```python
import math

import jax
import jax.numpy as jnp
import numpy as np
from jax import lax
from jax.experimental import pallas as pl
from jax.experimental.pallas import tpu as pltpu
from jax.sharding import PartitionSpec as P

LEVELS = 2
HIGH = lax.Precision.HIGHEST


def slot_tables(length):
    half = length // 2
    t = np.arange(length)
    q = np.arange(half)
    angle = 2.0 * np.pi * np.outer(q, t) / length
    fwd_re = np.cos(angle)
    fwd_im = -np.sin(angle)
    fwd_re[0] = 1.0
    fwd_im[0] = np.cos(np.pi * t)
    inv_re = 2.0 * np.cos(angle.T) / length
    inv_im = -2.0 * np.sin(angle.T) / length
    inv_re[:, 0] = 1.0 / length
    inv_im[:, 0] = np.cos(np.pi * t) / length
    fwd = np.concatenate([fwd_re, fwd_im], 0)
    inv = np.concatenate([inv_re, inv_im], 1)
    return jnp.asarray(fwd, jnp.float32), jnp.asarray(inv, jnp.float32)


def _products_body(pick_ref, src_ref, row_ref, mine_ref, other_ref, kk_ref, out_ref):
    out_ref[...] = jnp.zeros_like(out_ref)

    def step(k, carry):
        p = pick_ref[k]
        x = jnp.where(src_ref[k] == 1, other_ref[p], mine_ref[p])
        prod = lax.dot_general(
            x, kk_ref[k], (((1,), (1,)), ((), ())), preferred_element_type=jnp.float32
        )
        r = row_ref[k]
        out_ref[r] = out_ref[r] + prod
        return carry

    lax.fori_loop(0, kk_ref.shape[0], step, 0, unroll=16)


def block_products(pick, src, row, mine, other, kk, rows_local):
    nblk, m, j = mine.shape
    nnz, n, _ = kk.shape
    full = lambda *shape: pl.BlockSpec(shape, lambda i, *_: (0,) * len(shape))
    return pl.pallas_call(
        _products_body,
        grid_spec=pltpu.PrefetchScalarGridSpec(
            num_scalar_prefetch=3,
            grid=(1,),
            in_specs=[full(nblk, m, j), full(nblk, m, j), full(nnz, n, j)],
            out_specs=full(rows_local, m, n),
        ),
        out_shape=jax.ShapeDtypeStruct((rows_local, m, n), jnp.float32),
    )(pick, src, row, mine, other, kk)


def shards(solution, kernel, pattern, offsets):
    ntm = lax.axis_size("tm")
    nst = lax.axis_size("state")
    length = solution.shape[0] * ntm
    half = length // 2
    per_slot = ntm // half
    cols = solution.shape[1]
    states_local = solution.shape[2]
    nnz, _, block, _ = kernel.shape
    rows_local = states_local // block
    csl = cols // ntm
    sh = states_local // per_slot
    fwd_table, inv_table = slot_tables(length)

    me = lax.axis_index("tm")
    my_state = lax.axis_index("state")
    my_slot = me // per_slot
    my_half = me % per_slot
    swap = [(i, i ^ 1) for i in range(ntm)]

    rows_dev = block // (per_slot * ntm)
    ksrc = kernel[:, 0].reshape(nnz, per_slot, ntm, rows_dev, block)
    ksrc = jnp.transpose(ksrc, (2, 1, 0, 3, 4)).reshape(ntm, -1, block)
    klags = lax.all_to_all(ksrc, "tm", 0, 0, tiled=True).astype(jnp.float32)
    klags = klags.reshape(length, per_slot, nnz * rows_dev, block)
    kspec = jnp.einsum(
        "xqt,thrj->qhxrj", fwd_table.reshape(2, half, length), klags, precision=HIGH
    ).astype(jnp.bfloat16)
    kspec = kspec.reshape(ntm, -1, block)
    kspec = lax.all_to_all(kspec, "tm", 0, 0, tiled=True)
    kspec = kspec.reshape(ntm, 2, nnz, rows_dev, block)
    kk = jnp.transpose(kspec, (2, 1, 0, 3, 4)).reshape(nnz, block, block)
    local_rows = pattern[:, 0] - my_state * rows_local
    row_of = jnp.clip(local_rows, 0, rows_local - 1)
    real_slot = (my_slot != 0).astype(jnp.float32)

    col_block = pattern[:, 1]
    blocks_half = rows_local // per_slot
    rel = (col_block // rows_local - my_state) % nst
    rel = jnp.where(rel < nst // 2, rel, rel - nst)
    position = jnp.where(rel > 0, 2 * rel, -2 * rel - 1)
    position = jnp.where(rel == 0, 0, position)
    cb_half = (col_block // blocks_half) % per_slot
    cb_src = (cb_half != my_half).astype(jnp.int32)
    pick = position * blocks_half + col_block % blocks_half
    fwd = [(i, (i + 1) % nst) for i in range(nst)]
    bwd = [(i, (i - 1) % nst) for i in range(nst)]

    def ring_gather(x):
        parts = [x]
        a = x
        b = x
        for step in range(1, nst // 2 + 1):
            a = lax.ppermute(a, "state", fwd)
            parts.append(a)
            if step < nst // 2:
                b = lax.ppermute(b, "state", bwd)
                parts.append(b)
        return jnp.concatenate(parts, 0)

    def respond(left):
        xs = jnp.einsum("qt,tcn->qcn", fwd_table, left, precision=HIGH).astype(jnp.bfloat16)
        xs = xs.reshape(2, half, csl, per_slot, blocks_half, block)
        xs = jnp.transpose(xs, (1, 3, 0, 2, 4, 5)).reshape(ntm, -1, block)
        xs = lax.all_to_all(xs, "tm", 0, 0, tiled=True)
        xs = xs.reshape(ntm, 2, csl, blocks_half, block)
        xs = jnp.transpose(xs, (3, 1, 0, 2, 4)).reshape(blocks_half, 2 * cols, block)
        mine = ring_gather(xs)
        other = lax.ppermute(mine, "tm", swap)
        prod = block_products(pick, cb_src, row_of, mine, other, kk, rows_local)
        ah = block // per_slot
        a, c_ = prod[:, :cols, :ah], prod[:, :cols, ah:]
        d, b = prod[:, cols:, :ah], prod[:, cols:, ah:]
        ys_re = a - real_slot * b
        ys_im = real_slot * (c_ + d) + (1.0 - real_slot) * b
        ys = jnp.stack([ys_re, ys_im], 0).reshape(2, rows_local, ntm, csl, ah)
        ys = jnp.transpose(ys, (2, 0, 3, 1, 4)).reshape(ntm, -1, 2 * ah)
        ys = lax.all_to_all(ys, "tm", 0, 0, tiled=True)
        ys = ys.reshape(half, per_slot, 2, csl, rows_local // 2, 2, ah)
        ys = jnp.transpose(ys, (2, 0, 3, 4, 5, 1, 6)).reshape(length, csl * rows_local, block)
        return jnp.einsum("tq,qcn->tcn", inv_table, ys, precision=HIGH)

    field = solution[0].reshape(ntm, csl * rows_local, block)
    field = lax.all_to_all(field, "tm", 0, 0, tiled=True)
    times = jnp.arange(length, dtype=jnp.int32)[:, None, None]
    for level_index in range(LEVELS):
        boundary = offsets[level_index]
        left = jnp.where(times < boundary, field, 0.0)
        response = respond(left)
        field = field + jnp.where(times >= boundary, response, 0.0)
    field = lax.all_to_all(field, "tm", 0, 0, tiled=True)
    return field.reshape(1, cols, states_local)


def solution(mesh):
    return jax.shard_map(
        shards,
        mesh=mesh,
        in_specs=(P("tm", None, "state"), P("state", "tm", None, None), P("state", None), P()),
        out_specs=P("tm", None, "state"),
        check_vma=False,
    )
```

```python
import math

import jax
import jax.numpy as jnp
import numpy as np
from jax import lax
from jax.experimental import pallas as pl
from jax.experimental.pallas import tpu as pltpu
from jax.sharding import PartitionSpec as P

LEVELS = 2
HIGH = lax.Precision.HIGHEST


def slot_tables(length):
    half = length // 2
    t = np.arange(length)
    q = np.arange(half)
    angle = 2.0 * np.pi * np.outer(q, t) / length
    fwd_re = np.cos(angle)
    fwd_im = -np.sin(angle)
    fwd_re[0] = 1.0
    fwd_im[0] = np.cos(np.pi * t)
    inv_re = 2.0 * np.cos(angle.T) / length
    inv_im = -2.0 * np.sin(angle.T) / length
    inv_re[:, 0] = 1.0 / length
    inv_im[:, 0] = np.cos(np.pi * t) / length
    fwd = np.concatenate([fwd_re, fwd_im], 0)
    inv = np.concatenate([inv_re, inv_im], 1)
    return jnp.asarray(fwd, jnp.float32), jnp.asarray(inv, jnp.float32)


def _products_body(pick_ref, src_ref, row_ref, mine_ref, other_ref, kk_ref, out_ref):
    out_ref[...] = jnp.zeros_like(out_ref)

    def step(k, carry):
        p = pick_ref[k]
        x = jnp.where(src_ref[k] == 1, other_ref[p], mine_ref[p])
        prod = lax.dot_general(
            x, kk_ref[k], (((1,), (1,)), ((), ())), preferred_element_type=jnp.float32
        )
        r = row_ref[k]
        out_ref[r] = out_ref[r] + prod
        return carry

    lax.fori_loop(0, kk_ref.shape[0], step, 0, unroll=16)


def block_products(pick, src, row, mine, other, kk, rows_local):
    nblk, m, j = mine.shape
    nnz, n, _ = kk.shape
    full = lambda *shape: pl.BlockSpec(shape, lambda i, *_: (0,) * len(shape))
    return pl.pallas_call(
        _products_body,
        grid_spec=pltpu.PrefetchScalarGridSpec(
            num_scalar_prefetch=3,
            grid=(1,),
            in_specs=[full(nblk, m, j), full(nblk, m, j), full(nnz, n, j)],
            out_specs=full(rows_local, m, n),
        ),
        out_shape=jax.ShapeDtypeStruct((rows_local, m, n), jnp.float32),
    )(pick, src, row, mine, other, kk)


def shards(solution, kernel, pattern, offsets):
    ntm = lax.axis_size("tm")
    nst = lax.axis_size("state")
    length = solution.shape[0] * ntm
    half = length // 2
    per_slot = ntm // half
    cols = solution.shape[1]
    states_local = solution.shape[2]
    nnz, _, block, _ = kernel.shape
    rows_local = states_local // block
    csl = cols // ntm
    sh = states_local // per_slot
    fwd_table, inv_table = slot_tables(length)

    me = lax.axis_index("tm")
    my_state = lax.axis_index("state")
    my_slot = me // per_slot
    my_half = me % per_slot
    swap = [(i, i ^ 1) for i in range(ntm)]

    rows_dev = block // (per_slot * ntm)
    ksrc = kernel[:, 0].reshape(nnz, per_slot, ntm, rows_dev, block)
    ksrc = jnp.transpose(ksrc, (2, 1, 0, 3, 4)).reshape(ntm, -1, block)
    field = solution[0].reshape(ntm, csl * rows_local, block)
    field = lax.all_to_all(field, "tm", 0, 0, tiled=True)
    field, ksrc = lax.optimization_barrier((field, ksrc))
    klags = lax.all_to_all(ksrc, "tm", 0, 0, tiled=True).astype(jnp.float32)
    klags = klags.reshape(length, per_slot, nnz * rows_dev, block)
    kspec = jnp.einsum(
        "xqt,thrj->qhxrj", fwd_table.reshape(2, half, length), klags, precision=HIGH
    ).astype(jnp.bfloat16)
    kspec = kspec.reshape(ntm, -1, block)
    kspec = lax.all_to_all(kspec, "tm", 0, 0, tiled=True)
    kspec = kspec.reshape(ntm, 2, nnz, rows_dev, block)
    kk = jnp.transpose(kspec, (2, 1, 0, 3, 4)).reshape(nnz, block, block)
    local_rows = pattern[:, 0] - my_state * rows_local
    row_of = jnp.clip(local_rows, 0, rows_local - 1)
    real_slot = (my_slot != 0).astype(jnp.float32)

    col_block = pattern[:, 1]
    blocks_half = rows_local // per_slot
    rel = (col_block // rows_local - my_state) % nst
    rel = jnp.where(rel < nst // 2, rel, rel - nst)
    position = jnp.where(rel > 0, 2 * rel, -2 * rel - 1)
    position = jnp.where(rel == 0, 0, position)
    cb_half = (col_block // blocks_half) % per_slot
    cb_src = (cb_half != my_half).astype(jnp.int32)
    pick = position * blocks_half + col_block % blocks_half
    fwd = [(i, (i + 1) % nst) for i in range(nst)]
    bwd = [(i, (i - 1) % nst) for i in range(nst)]

    def ring_gather(x):
        parts = [x]
        a = x
        b = x
        for step in range(1, nst // 2 + 1):
            a = lax.ppermute(a, "state", fwd)
            parts.append(a)
            if step < nst // 2:
                b = lax.ppermute(b, "state", bwd)
                parts.append(b)
        return jnp.concatenate(parts, 0)

    def respond(left):
        xs = jnp.einsum("qt,tcn->qcn", fwd_table, left, precision=HIGH).astype(jnp.bfloat16)
        xs = xs.reshape(2, half, csl, per_slot, blocks_half, block)
        xs = jnp.transpose(xs, (1, 3, 0, 2, 4, 5)).reshape(ntm, -1, block)
        xs = lax.all_to_all(xs, "tm", 0, 0, tiled=True)
        xs = xs.reshape(ntm, 2, csl, blocks_half, block)
        xs = jnp.transpose(xs, (3, 1, 0, 2, 4)).reshape(blocks_half, 2 * cols, block)
        mine = ring_gather(xs)
        other = lax.ppermute(mine, "tm", swap)
        prod = block_products(pick, cb_src, row_of, mine, other, kk, rows_local)
        ah = block // per_slot
        a, c_ = prod[:, :cols, :ah], prod[:, :cols, ah:]
        d, b = prod[:, cols:, :ah], prod[:, cols:, ah:]
        ys_re = a - real_slot * b
        ys_im = real_slot * (c_ + d) + (1.0 - real_slot) * b
        ys = jnp.stack([ys_re, ys_im], 0).reshape(2, rows_local, ntm, csl, ah)
        ys = jnp.transpose(ys, (2, 0, 3, 1, 4)).reshape(ntm, -1, 2 * ah)
        ys = lax.all_to_all(ys, "tm", 0, 0, tiled=True)
        ys = ys.reshape(half, per_slot, 2, csl, rows_local // 2, 2, ah)
        ys = jnp.transpose(ys, (2, 0, 3, 4, 5, 1, 6)).reshape(length, csl * rows_local, block)
        return jnp.einsum("tq,qcn->tcn", inv_table, ys, precision=HIGH)

    times = jnp.arange(length, dtype=jnp.int32)[:, None, None]
    for level_index in range(LEVELS):
        boundary = offsets[level_index]
        left = jnp.where(times < boundary, field, 0.0)
        response = respond(left)
        field = field + jnp.where(times >= boundary, response, 0.0)
    field = lax.all_to_all(field, "tm", 0, 0, tiled=True)
    return field.reshape(1, cols, states_local)


def solution(mesh):
    return jax.shard_map(
        shards,
        mesh=mesh,
        in_specs=(P("tm", None, "state"), P("state", "tm", None, None), P("state", None), P()),
        out_specs=P("tm", None, "state"),
        check_vma=False,
    )
```

```python
import math

import jax
import jax.numpy as jnp
import numpy as np
from jax import lax
from jax.experimental import pallas as pl
from jax.experimental.pallas import tpu as pltpu
from jax.sharding import PartitionSpec as P

LEVELS = 2
HIGH = lax.Precision.HIGHEST


def slot_tables(length):
    half = length // 2
    t = np.arange(length)
    q = np.arange(half)
    angle = 2.0 * np.pi * np.outer(q, t) / length
    fwd_re = np.cos(angle)
    fwd_im = -np.sin(angle)
    fwd_re[0] = 1.0
    fwd_im[0] = np.cos(np.pi * t)
    inv_re = 2.0 * np.cos(angle.T) / length
    inv_im = -2.0 * np.sin(angle.T) / length
    inv_re[:, 0] = 1.0 / length
    inv_im[:, 0] = np.cos(np.pi * t) / length
    fwd = np.concatenate([fwd_re, fwd_im], 0)
    inv = np.concatenate([inv_re, inv_im], 1)
    return jnp.asarray(fwd, jnp.float32), jnp.asarray(inv, jnp.float32)


def _products_body(pick_ref, src_ref, row_ref, mine_ref, other_ref, kk_ref, out_ref):
    out_ref[...] = jnp.zeros_like(out_ref)

    def step(k, carry):
        p = pick_ref[k]
        x = jnp.where(src_ref[k] == 1, other_ref[p], mine_ref[p])
        prod = lax.dot_general(
            x, kk_ref[k], (((1,), (1,)), ((), ())), preferred_element_type=jnp.float32
        )
        r = row_ref[k]
        out_ref[r] = out_ref[r] + prod
        return carry

    lax.fori_loop(0, kk_ref.shape[0], step, 0, unroll=16)


def block_products(pick, src, row, mine, other, kk, rows_local):
    nblk, m, j = mine.shape
    nnz, n, _ = kk.shape
    full = lambda *shape: pl.BlockSpec(shape, lambda i, *_: (0,) * len(shape))
    return pl.pallas_call(
        _products_body,
        grid_spec=pltpu.PrefetchScalarGridSpec(
            num_scalar_prefetch=3,
            grid=(1,),
            in_specs=[full(nblk, m, j), full(nblk, m, j), full(nnz, n, j)],
            out_specs=full(rows_local, m, n),
        ),
        out_shape=jax.ShapeDtypeStruct((rows_local, m, n), jnp.float32),
    )(pick, src, row, mine, other, kk)


def shards(solution, kernel, pattern, offsets):
    ntm = lax.axis_size("tm")
    nst = lax.axis_size("state")
    length = solution.shape[0] * ntm
    half = length // 2
    per_slot = ntm // half
    cols = solution.shape[1]
    states_local = solution.shape[2]
    nnz, _, block, _ = kernel.shape
    rows_local = states_local // block
    csl = cols // ntm
    sh = states_local // per_slot
    fwd_table, inv_table = slot_tables(length)

    me = lax.axis_index("tm")
    my_state = lax.axis_index("state")
    my_slot = me // per_slot
    my_half = me % per_slot
    swap = [(i, i ^ 1) for i in range(ntm)]

    rows_dev = block // (per_slot * ntm)
    ksrc = kernel[:, 0].reshape(nnz, per_slot, ntm, rows_dev, block)
    ksrc = jnp.transpose(ksrc, (2, 1, 0, 3, 4)).reshape(ntm, -1, block)
    field = solution[0].reshape(ntm, csl * rows_local, block)
    field = lax.all_to_all(field, "tm", 0, 0, tiled=True)
    field, ksrc = lax.optimization_barrier((field, ksrc))
    klags = lax.all_to_all(ksrc, "tm", 0, 0, tiled=True).astype(jnp.float32)
    klags = klags.reshape(length, per_slot, nnz * rows_dev, block)
    kspec = jnp.einsum(
        "xqt,thrj->qhxrj", fwd_table.reshape(2, half, length), klags, precision=HIGH
    ).astype(jnp.bfloat16)
    kspec = kspec.reshape(ntm, -1, block)
    kspec = lax.all_to_all(kspec, "tm", 0, 0, tiled=True)
    kspec = kspec.reshape(ntm, 2, nnz, rows_dev, block)
    kk = jnp.transpose(kspec, (2, 1, 0, 3, 4)).reshape(nnz, block, block)
    local_rows = pattern[:, 0] - my_state * rows_local
    row_of = jnp.clip(local_rows, 0, rows_local - 1)
    real_slot = (my_slot != 0).astype(jnp.float32)

    col_block = pattern[:, 1]
    blocks_half = rows_local // per_slot
    rel = (col_block // rows_local - my_state) % nst
    rel = jnp.where(rel < nst // 2, rel, rel - nst)
    position = jnp.where(rel > 0, 2 * rel, -2 * rel - 1)
    position = jnp.where(rel == 0, 0, position)
    cb_half = (col_block // blocks_half) % per_slot
    cb_src = (cb_half != my_half).astype(jnp.int32)
    pick = position * blocks_half + col_block % blocks_half
    fwd = [(i, (i + 1) % nst) for i in range(nst)]
    bwd = [(i, (i - 1) % nst) for i in range(nst)]

    def ring_gather(x):
        parts = [x]
        a = x
        b = x
        for step in range(1, nst // 2 + 1):
            a = lax.ppermute(a, "state", fwd)
            parts.append(a)
            if step < nst // 2:
                b = lax.ppermute(b, "state", bwd)
                parts.append(b)
        return jnp.concatenate(parts, 0)

    def respond(left):
        xs = jnp.einsum("qt,tcn->qcn", fwd_table, left, precision=HIGH).astype(jnp.bfloat16)
        xs = xs.reshape(2, half, csl, per_slot, blocks_half, block)
        xs = jnp.transpose(xs, (1, 3, 0, 2, 4, 5)).reshape(ntm, -1, block)
        xs = lax.all_to_all(xs, "tm", 0, 0, tiled=True)
        xs = xs.reshape(ntm, 2, csl, blocks_half, block)
        xs = jnp.transpose(xs, (3, 1, 0, 2, 4)).reshape(blocks_half, 2 * cols, block)
        mine = ring_gather(xs)
        other = lax.ppermute(mine, "tm", swap)
        prod = block_products(pick, cb_src, row_of, mine, other, kk, rows_local)
        ah = block // per_slot
        a, c_ = prod[:, :cols, :ah], prod[:, :cols, ah:]
        d, b = prod[:, cols:, :ah], prod[:, cols:, ah:]
        ys_re = a - real_slot * b
        ys_im = real_slot * (c_ + d) + (1.0 - real_slot) * b
        ys = jnp.stack([ys_re, ys_im], 0).reshape(2, rows_local, ntm, csl, ah)
        ys = jnp.transpose(ys, (2, 0, 3, 1, 4)).reshape(ntm, -1, 2 * ah).astype(jnp.bfloat16)
        ys = lax.all_to_all(ys, "tm", 0, 0, tiled=True).astype(jnp.float32)
        ys = ys.reshape(half, per_slot, 2, csl, rows_local // 2, 2, ah)
        ys = jnp.transpose(ys, (2, 0, 3, 4, 5, 1, 6)).reshape(length, csl * rows_local, block)
        return jnp.einsum("tq,qcn->tcn", inv_table, ys, precision=HIGH)

    times = jnp.arange(length, dtype=jnp.int32)[:, None, None]
    for level_index in range(LEVELS):
        boundary = offsets[level_index]
        left = jnp.where(times < boundary, field, 0.0)
        response = respond(left)
        field = field + jnp.where(times >= boundary, response, 0.0)
    field = lax.all_to_all(field, "tm", 0, 0, tiled=True)
    return field.reshape(1, cols, states_local)


def solution(mesh):
    return jax.shard_map(
        shards,
        mesh=mesh,
        in_specs=(P("tm", None, "state"), P("state", "tm", None, None), P("state", None), P()),
        out_specs=P("tm", None, "state"),
        check_vma=False,
    )
```

```python
import math

import jax
import jax.numpy as jnp
import numpy as np
from jax import lax
from jax.experimental import pallas as pl
from jax.experimental.pallas import tpu as pltpu
from jax.sharding import PartitionSpec as P

LEVELS = 2
HIGH = lax.Precision.HIGHEST


def slot_tables(length):
    half = length // 2
    t = np.arange(length)
    q = np.arange(half)
    angle = 2.0 * np.pi * np.outer(q, t) / length
    fwd_re = np.cos(angle)
    fwd_im = -np.sin(angle)
    fwd_re[0] = 1.0
    fwd_im[0] = np.cos(np.pi * t)
    inv_re = 2.0 * np.cos(angle.T) / length
    inv_im = -2.0 * np.sin(angle.T) / length
    inv_re[:, 0] = 1.0 / length
    inv_im[:, 0] = np.cos(np.pi * t) / length
    fwd = np.concatenate([fwd_re, fwd_im], 0)
    inv = np.concatenate([inv_re, inv_im], 1)
    return jnp.asarray(fwd, jnp.float32), jnp.asarray(inv, jnp.float32)


def _products_body(pick_ref, src_ref, row_ref, mine_ref, other_ref, kk_ref, out_ref):
    out_ref[...] = jnp.zeros_like(out_ref)

    def step(k, carry):
        p = pick_ref[k]
        x = lax.cond(src_ref[k] == 1, lambda: other_ref[p], lambda: mine_ref[p])
        prod = lax.dot_general(
            x, kk_ref[k], (((1,), (1,)), ((), ())), preferred_element_type=jnp.float32
        )
        r = row_ref[k]
        out_ref[r] = out_ref[r] + prod
        return carry

    lax.fori_loop(0, kk_ref.shape[0], step, 0, unroll=16)


def block_products(pick, src, row, mine, other, kk, rows_local):
    nblk, m, j = mine.shape
    nnz, n, _ = kk.shape
    full = lambda *shape: pl.BlockSpec(shape, lambda i, *_: (0,) * len(shape))
    return pl.pallas_call(
        _products_body,
        grid_spec=pltpu.PrefetchScalarGridSpec(
            num_scalar_prefetch=3,
            grid=(1,),
            in_specs=[full(nblk, m, j), full(nblk, m, j), full(nnz, n, j)],
            out_specs=full(rows_local, m, n),
        ),
        out_shape=jax.ShapeDtypeStruct((rows_local, m, n), jnp.float32),
    )(pick, src, row, mine, other, kk)


def shards(solution, kernel, pattern, offsets):
    ntm = lax.axis_size("tm")
    nst = lax.axis_size("state")
    length = solution.shape[0] * ntm
    half = length // 2
    per_slot = ntm // half
    cols = solution.shape[1]
    states_local = solution.shape[2]
    nnz, _, block, _ = kernel.shape
    rows_local = states_local // block
    csl = cols // ntm
    sh = states_local // per_slot
    fwd_table, inv_table = slot_tables(length)

    me = lax.axis_index("tm")
    my_state = lax.axis_index("state")
    my_slot = me // per_slot
    my_half = me % per_slot
    swap = [(i, i ^ 1) for i in range(ntm)]

    rows_dev = block // (per_slot * ntm)
    ksrc = kernel[:, 0].reshape(nnz, per_slot, ntm, rows_dev, block)
    ksrc = jnp.transpose(ksrc, (2, 1, 0, 3, 4)).reshape(ntm, -1, block)
    field = solution[0].reshape(ntm, csl * rows_local, block)
    field = lax.all_to_all(field, "tm", 0, 0, tiled=True)
    field, ksrc = lax.optimization_barrier((field, ksrc))
    klags = lax.all_to_all(ksrc, "tm", 0, 0, tiled=True).astype(jnp.float32)
    klags = klags.reshape(length, per_slot, nnz * rows_dev, block)
    kspec = jnp.einsum(
        "xqt,thrj->qhxrj", fwd_table.reshape(2, half, length), klags, precision=HIGH
    ).astype(jnp.bfloat16)
    kspec = kspec.reshape(ntm, -1, block)
    kspec = lax.all_to_all(kspec, "tm", 0, 0, tiled=True)
    kspec = kspec.reshape(ntm, 2, nnz, rows_dev, block)
    kk = jnp.transpose(kspec, (2, 1, 0, 3, 4)).reshape(nnz, block, block)
    local_rows = pattern[:, 0] - my_state * rows_local
    row_of = jnp.clip(local_rows, 0, rows_local - 1)
    real_slot = (my_slot != 0).astype(jnp.float32)

    col_block = pattern[:, 1]
    blocks_half = rows_local // per_slot
    rel = (col_block // rows_local - my_state) % nst
    rel = jnp.where(rel < nst // 2, rel, rel - nst)
    position = jnp.where(rel > 0, 2 * rel, -2 * rel - 1)
    position = jnp.where(rel == 0, 0, position)
    cb_half = (col_block // blocks_half) % per_slot
    cb_src = (cb_half != my_half).astype(jnp.int32)
    pick = position * blocks_half + col_block % blocks_half
    fwd = [(i, (i + 1) % nst) for i in range(nst)]
    bwd = [(i, (i - 1) % nst) for i in range(nst)]

    def ring_gather(x):
        parts = [x]
        a = x
        b = x
        for step in range(1, nst // 2 + 1):
            a = lax.ppermute(a, "state", fwd)
            parts.append(a)
            if step < nst // 2:
                b = lax.ppermute(b, "state", bwd)
                parts.append(b)
        return jnp.concatenate(parts, 0)

    def respond(left):
        xs = jnp.einsum("qt,tcn->qcn", fwd_table, left, precision=HIGH).astype(jnp.bfloat16)
        xs = xs.reshape(2, half, csl, per_slot, blocks_half, block)
        xs = jnp.transpose(xs, (1, 3, 0, 2, 4, 5)).reshape(ntm, -1, block)
        xs = lax.all_to_all(xs, "tm", 0, 0, tiled=True)
        xs = xs.reshape(ntm, 2, csl, blocks_half, block)
        xs = jnp.transpose(xs, (3, 1, 0, 2, 4)).reshape(blocks_half, 2 * cols, block)
        mine = ring_gather(xs)
        other = lax.ppermute(mine, "tm", swap)
        prod = block_products(pick, cb_src, row_of, mine, other, kk, rows_local)
        ah = block // per_slot
        a, c_ = prod[:, :cols, :ah], prod[:, :cols, ah:]
        d, b = prod[:, cols:, :ah], prod[:, cols:, ah:]
        ys_re = a - real_slot * b
        ys_im = real_slot * (c_ + d) + (1.0 - real_slot) * b
        ys = jnp.stack([ys_re, ys_im], 0).reshape(2, rows_local, ntm, csl, ah)
        ys = jnp.transpose(ys, (2, 0, 3, 1, 4)).reshape(ntm, -1, 2 * ah)
        ys = lax.all_to_all(ys, "tm", 0, 0, tiled=True)
        ys = ys.reshape(half, per_slot, 2, csl, rows_local // 2, 2, ah)
        ys = jnp.transpose(ys, (2, 0, 3, 4, 5, 1, 6)).reshape(length, csl * rows_local, block)
        return jnp.einsum("tq,qcn->tcn", inv_table, ys, precision=HIGH)

    times = jnp.arange(length, dtype=jnp.int32)[:, None, None]
    for level_index in range(LEVELS):
        boundary = offsets[level_index]
        left = jnp.where(times < boundary, field, 0.0)
        response = respond(left)
        field = field + jnp.where(times >= boundary, response, 0.0)
    field = lax.all_to_all(field, "tm", 0, 0, tiled=True)
    return field.reshape(1, cols, states_local)


def solution(mesh):
    return jax.shard_map(
        shards,
        mesh=mesh,
        in_specs=(P("tm", None, "state"), P("state", "tm", None, None), P("state", None), P()),
        out_specs=P("tm", None, "state"),
        check_vma=False,
    )
```

```python
import math

import jax
import jax.numpy as jnp
import numpy as np
from jax import lax
from jax.experimental import pallas as pl
from jax.experimental.pallas import tpu as pltpu
from jax.sharding import PartitionSpec as P

LEVELS = 2
HIGH = lax.Precision.HIGHEST


def slot_tables(length):
    half = length // 2
    t = np.arange(length)
    q = np.arange(half)
    angle = 2.0 * np.pi * np.outer(q, t) / length
    fwd_re = np.cos(angle)
    fwd_im = -np.sin(angle)
    fwd_re[0] = 1.0
    fwd_im[0] = np.cos(np.pi * t)
    inv_re = 2.0 * np.cos(angle.T) / length
    inv_im = -2.0 * np.sin(angle.T) / length
    inv_re[:, 0] = 1.0 / length
    inv_im[:, 0] = np.cos(np.pi * t) / length
    fwd = np.concatenate([fwd_re, fwd_im], 0)
    inv = np.concatenate([inv_re, inv_im], 1)
    return jnp.asarray(fwd, jnp.float32), jnp.asarray(inv, jnp.float32)


def _products_body(pick_ref, src_ref, row_ref, mine_ref, other_ref, kk_ref, out_ref):
    out_ref[...] = jnp.zeros_like(out_ref)

    def step(k, carry):
        p = pick_ref[k]
        x = jnp.where(src_ref[k] == 1, other_ref[p], mine_ref[p])
        prod = lax.dot_general(
            x, kk_ref[k], (((1,), (1,)), ((), ())), preferred_element_type=jnp.float32
        )
        r = row_ref[k]
        out_ref[r] = out_ref[r] + prod
        return carry

    lax.fori_loop(0, kk_ref.shape[0], step, 0, unroll=True)


def block_products(pick, src, row, mine, other, kk, rows_local):
    nblk, m, j = mine.shape
    nnz, n, _ = kk.shape
    full = lambda *shape: pl.BlockSpec(shape, lambda i, *_: (0,) * len(shape))
    return pl.pallas_call(
        _products_body,
        grid_spec=pltpu.PrefetchScalarGridSpec(
            num_scalar_prefetch=3,
            grid=(1,),
            in_specs=[full(nblk, m, j), full(nblk, m, j), full(nnz, n, j)],
            out_specs=full(rows_local, m, n),
        ),
        out_shape=jax.ShapeDtypeStruct((rows_local, m, n), jnp.float32),
    )(pick, src, row, mine, other, kk)


def shards(solution, kernel, pattern, offsets):
    ntm = lax.axis_size("tm")
    nst = lax.axis_size("state")
    length = solution.shape[0] * ntm
    half = length // 2
    per_slot = ntm // half
    cols = solution.shape[1]
    states_local = solution.shape[2]
    nnz, _, block, _ = kernel.shape
    rows_local = states_local // block
    csl = cols // ntm
    sh = states_local // per_slot
    fwd_table, inv_table = slot_tables(length)

    me = lax.axis_index("tm")
    my_state = lax.axis_index("state")
    my_slot = me // per_slot
    my_half = me % per_slot
    swap = [(i, i ^ 1) for i in range(ntm)]

    rows_dev = block // (per_slot * ntm)
    ksrc = kernel[:, 0].reshape(nnz, per_slot, ntm, rows_dev, block)
    ksrc = jnp.transpose(ksrc, (2, 1, 0, 3, 4)).reshape(ntm, -1, block)
    field = solution[0].reshape(ntm, csl * rows_local, block)
    field = lax.all_to_all(field, "tm", 0, 0, tiled=True)
    field, ksrc = lax.optimization_barrier((field, ksrc))
    klags = lax.all_to_all(ksrc, "tm", 0, 0, tiled=True).astype(jnp.float32)
    klags = klags.reshape(length, per_slot, nnz * rows_dev, block)
    kspec = jnp.einsum(
        "xqt,thrj->qhxrj", fwd_table.reshape(2, half, length), klags, precision=HIGH
    ).astype(jnp.bfloat16)
    kspec = kspec.reshape(ntm, -1, block)
    kspec = lax.all_to_all(kspec, "tm", 0, 0, tiled=True)
    kspec = kspec.reshape(ntm, 2, nnz, rows_dev, block)
    kk = jnp.transpose(kspec, (2, 1, 0, 3, 4)).reshape(nnz, block, block)
    local_rows = pattern[:, 0] - my_state * rows_local
    row_of = jnp.clip(local_rows, 0, rows_local - 1)
    real_slot = (my_slot != 0).astype(jnp.float32)

    col_block = pattern[:, 1]
    blocks_half = rows_local // per_slot
    rel = (col_block // rows_local - my_state) % nst
    rel = jnp.where(rel < nst // 2, rel, rel - nst)
    position = jnp.where(rel > 0, 2 * rel, -2 * rel - 1)
    position = jnp.where(rel == 0, 0, position)
    cb_half = (col_block // blocks_half) % per_slot
    cb_src = (cb_half != my_half).astype(jnp.int32)
    pick = position * blocks_half + col_block % blocks_half
    fwd = [(i, (i + 1) % nst) for i in range(nst)]
    bwd = [(i, (i - 1) % nst) for i in range(nst)]

    def ring_gather(x):
        parts = [x]
        a = x
        b = x
        for step in range(1, nst // 2 + 1):
            a = lax.ppermute(a, "state", fwd)
            parts.append(a)
            if step < nst // 2:
                b = lax.ppermute(b, "state", bwd)
                parts.append(b)
        return jnp.concatenate(parts, 0)

    def respond(left):
        xs = jnp.einsum("qt,tcn->qcn", fwd_table, left, precision=HIGH).astype(jnp.bfloat16)
        xs = xs.reshape(2, half, csl, per_slot, blocks_half, block)
        xs = jnp.transpose(xs, (1, 3, 0, 2, 4, 5)).reshape(ntm, -1, block)
        xs = lax.all_to_all(xs, "tm", 0, 0, tiled=True)
        xs = xs.reshape(ntm, 2, csl, blocks_half, block)
        xs = jnp.transpose(xs, (3, 1, 0, 2, 4)).reshape(blocks_half, 2 * cols, block)
        mine = ring_gather(xs)
        other = lax.ppermute(mine, "tm", swap)
        prod = block_products(pick, cb_src, row_of, mine, other, kk, rows_local)
        ah = block // per_slot
        a, c_ = prod[:, :cols, :ah], prod[:, :cols, ah:]
        d, b = prod[:, cols:, :ah], prod[:, cols:, ah:]
        ys_re = a - real_slot * b
        ys_im = real_slot * (c_ + d) + (1.0 - real_slot) * b
        ys = jnp.stack([ys_re, ys_im], 0).reshape(2, rows_local, ntm, csl, ah)
        ys = jnp.transpose(ys, (2, 0, 3, 1, 4)).reshape(ntm, -1, 2 * ah)
        ys = lax.all_to_all(ys, "tm", 0, 0, tiled=True)
        ys = ys.reshape(half, per_slot, 2, csl, rows_local // 2, 2, ah)
        ys = jnp.transpose(ys, (2, 0, 3, 4, 5, 1, 6)).reshape(length, csl * rows_local, block)
        return jnp.einsum("tq,qcn->tcn", inv_table, ys, precision=HIGH)

    times = jnp.arange(length, dtype=jnp.int32)[:, None, None]
    for level_index in range(LEVELS):
        boundary = offsets[level_index]
        left = jnp.where(times < boundary, field, 0.0)
        response = respond(left)
        field = field + jnp.where(times >= boundary, response, 0.0)
    field = lax.all_to_all(field, "tm", 0, 0, tiled=True)
    return field.reshape(1, cols, states_local)


def solution(mesh):
    return jax.shard_map(
        shards,
        mesh=mesh,
        in_specs=(P("tm", None, "state"), P("state", "tm", None, None), P("state", None), P()),
        out_specs=P("tm", None, "state"),
        check_vma=False,
    )
```

```python
import math

import jax
import jax.numpy as jnp
import numpy as np
from jax import lax
from jax.experimental import pallas as pl
from jax.experimental.pallas import tpu as pltpu
from jax.sharding import PartitionSpec as P

LEVELS = 2
HIGH = lax.Precision.HIGHEST


def slot_tables(length):
    half = length // 2
    t = np.arange(length)
    q = np.arange(half)
    angle = 2.0 * np.pi * np.outer(q, t) / length
    fwd_re = np.cos(angle)
    fwd_im = -np.sin(angle)
    fwd_re[0] = 1.0
    fwd_im[0] = np.cos(np.pi * t)
    inv_re = 2.0 * np.cos(angle.T) / length
    inv_im = -2.0 * np.sin(angle.T) / length
    inv_re[:, 0] = 1.0 / length
    inv_im[:, 0] = np.cos(np.pi * t) / length
    fwd = np.concatenate([fwd_re, fwd_im], 0)
    inv = np.concatenate([inv_re, inv_im], 1)
    return jnp.asarray(fwd, jnp.float32), jnp.asarray(inv, jnp.float32)


def _products_body(pick_ref, src_ref, row_ref, mine_ref, other_ref, kk_ref, out_ref):
    out_ref[...] = jnp.zeros_like(out_ref)

    def step(k, carry):
        p = pick_ref[k]
        x = jnp.where(src_ref[k] == 1, other_ref[p], mine_ref[p])
        prod = lax.dot_general(
            x, kk_ref[k], (((1,), (1,)), ((), ())), preferred_element_type=jnp.float32
        )
        r = row_ref[k]
        out_ref[r] = out_ref[r] + prod
        return carry

    lax.fori_loop(0, kk_ref.shape[0], step, 0, unroll=True)


def block_products(pick, src, row, mine, other, kk, rows_local):
    nblk, m, j = mine.shape
    nnz, n, _ = kk.shape
    full = lambda *shape: pl.BlockSpec(shape, lambda i, *_: (0,) * len(shape))
    return pl.pallas_call(
        _products_body,
        grid_spec=pltpu.PrefetchScalarGridSpec(
            num_scalar_prefetch=3,
            grid=(1,),
            in_specs=[full(nblk, m, j), full(nblk, m, j), full(nnz, n, j)],
            out_specs=full(rows_local, m, n),
        ),
        out_shape=jax.ShapeDtypeStruct((rows_local, m, n), jnp.float32),
    )(pick, src, row, mine, other, kk)


def shards(solution, kernel, pattern, offsets):
    ntm = lax.axis_size("tm")
    nst = lax.axis_size("state")
    length = solution.shape[0] * ntm
    half = length // 2
    per_slot = ntm // half
    cols = solution.shape[1]
    states_local = solution.shape[2]
    nnz, _, block, _ = kernel.shape
    rows_local = states_local // block
    csl = cols // ntm
    sh = states_local // per_slot
    fwd_table, inv_table = slot_tables(length)

    me = lax.axis_index("tm")
    my_state = lax.axis_index("state")
    my_slot = me // per_slot
    my_half = me % per_slot
    swap = [(i, i ^ 1) for i in range(ntm)]

    rows_dev = block // (per_slot * ntm)
    ksrc = kernel[:, 0].reshape(nnz, per_slot, ntm, rows_dev, block)
    ksrc = jnp.transpose(ksrc, (2, 1, 0, 3, 4)).reshape(ntm, -1, block)
    field = solution[0].reshape(ntm, csl * rows_local, block)
    field = lax.all_to_all(field, "tm", 0, 0, tiled=True)
    field, ksrc = lax.optimization_barrier((field, ksrc))
    klags = lax.all_to_all(ksrc, "tm", 0, 0, tiled=True).astype(jnp.float32)
    klags = klags.reshape(length, per_slot, nnz * rows_dev, block)
    kspec = jnp.einsum(
        "xqt,thrj->qhxrj", fwd_table.reshape(2, half, length), klags, precision=HIGH
    ).astype(jnp.bfloat16)
    kspec = kspec.reshape(ntm, 2, nnz, 1, rows_dev, block)
    kspec = jnp.transpose(kspec, (0, 2, 1, 3, 4, 5))
    kspec = lax.all_to_all(kspec, "tm", 0, 3, tiled=True)
    kk = kspec.reshape(nnz, block, block)
    local_rows = pattern[:, 0] - my_state * rows_local
    row_of = jnp.clip(local_rows, 0, rows_local - 1)
    real_slot = (my_slot != 0).astype(jnp.float32)

    col_block = pattern[:, 1]
    blocks_half = rows_local // per_slot
    rel = (col_block // rows_local - my_state) % nst
    rel = jnp.where(rel < nst // 2, rel, rel - nst)
    position = jnp.where(rel > 0, 2 * rel, -2 * rel - 1)
    position = jnp.where(rel == 0, 0, position)
    cb_half = (col_block // blocks_half) % per_slot
    cb_src = (cb_half != my_half).astype(jnp.int32)
    pick = position * blocks_half + col_block % blocks_half
    fwd = [(i, (i + 1) % nst) for i in range(nst)]
    bwd = [(i, (i - 1) % nst) for i in range(nst)]

    def ring_gather(x):
        parts = [x]
        a = x
        b = x
        for step in range(1, nst // 2 + 1):
            a = lax.ppermute(a, "state", fwd)
            parts.append(a)
            if step < nst // 2:
                b = lax.ppermute(b, "state", bwd)
                parts.append(b)
        return jnp.concatenate(parts, 0)

    def respond(left):
        xs = jnp.einsum("qt,tcn->qcn", fwd_table, left, precision=HIGH).astype(jnp.bfloat16)
        xs = xs.reshape(2, half, csl, per_slot, blocks_half, block)
        xs = jnp.transpose(xs, (1, 3, 0, 2, 4, 5)).reshape(ntm, -1, block)
        xs = lax.all_to_all(xs, "tm", 0, 0, tiled=True)
        xs = xs.reshape(ntm, 2, csl, blocks_half, block)
        xs = jnp.transpose(xs, (3, 1, 0, 2, 4)).reshape(blocks_half, 2 * cols, block)
        mine = ring_gather(xs)
        other = lax.ppermute(mine, "tm", swap)
        prod = block_products(pick, cb_src, row_of, mine, other, kk, rows_local)
        ah = block // per_slot
        a, c_ = prod[:, :cols, :ah], prod[:, :cols, ah:]
        d, b = prod[:, cols:, :ah], prod[:, cols:, ah:]
        ys_re = a - real_slot * b
        ys_im = real_slot * (c_ + d) + (1.0 - real_slot) * b
        ys = jnp.stack([ys_re, ys_im], 0).reshape(2, rows_local, ntm, csl, ah)
        ys = jnp.transpose(ys, (2, 0, 3, 1, 4)).reshape(ntm, -1, 2 * ah)
        ys = lax.all_to_all(ys, "tm", 0, 0, tiled=True)
        ys = ys.reshape(half, per_slot, 2, csl, rows_local // 2, 2, ah)
        ys = jnp.transpose(ys, (2, 0, 3, 4, 5, 1, 6)).reshape(length, csl * rows_local, block)
        return jnp.einsum("tq,qcn->tcn", inv_table, ys, precision=HIGH)

    times = jnp.arange(length, dtype=jnp.int32)[:, None, None]
    for level_index in range(LEVELS):
        boundary = offsets[level_index]
        left = jnp.where(times < boundary, field, 0.0)
        response = respond(left)
        field = field + jnp.where(times >= boundary, response, 0.0)
    field = lax.all_to_all(field, "tm", 0, 0, tiled=True)
    return field.reshape(1, cols, states_local)


def solution(mesh):
    return jax.shard_map(
        shards,
        mesh=mesh,
        in_specs=(P("tm", None, "state"), P("state", "tm", None, None), P("state", None), P()),
        out_specs=P("tm", None, "state"),
        check_vma=False,
    )
```
